32 devices in a mesh: freq: 32 (over z, y, x, core), tm: 1.
Axes of the slice: x: 2, y: 2, z: 4, core: 2. Of those that a mesh axis runs over, the one named last changes fastest.
Arguments:
- voltages: int32 [1024, 8, 2, 4096], P('freq', 'tm'), may hold values from -127 to 127
- tile_map: int32 [36], replicated, may hold values from 0 to 35, each once
Outputs:
- visibilities: float32 [36, 64, 2, 128, 128], P('tm', 'freq')
The draws below stay inside these ranges and needn't reach their ends.
Inputs may be any that keep to these rules, and one draw needn't show every extreme that they name: `tile_map`: a permutation of the tile ids.
All inputs are finite; a program needn't handle non-finite values.
Results may differ from the reference program's by a relative error of at most 0.0052.
Values may be sent and summed in bfloat16 or wider, within the bound.
No kernel may reach another device: no remote copies, remote signals or barrier semaphores. Data moves between devices by JAX's collectives and lax.ppermute only.
A program may use at most 128 MiB of HBM per device.

```python
import math
import jax
import jax.numpy as jnp
from jax import lax

NCHAN = 4096
TAPS = 4
TB = 128
N_IN = 1024
SPECTRA = 8
CHANNELS = 64
FIRST = 2016
NTILES = 36


def touch_ends(array, rng, least, largest):
    place = [jax.random.randint(jax.random.fold_in(rng, axis), (), 0, length) for axis, length in enumerate(array.shape)]
    widest = array.shape.index(max(array.shape))
    beside = place[:widest] + [(place[widest] + 1) % array.shape[widest]] + place[widest + 1:]
    return array.at[tuple(place)].set(least).at[tuple(beside)].set(largest)


def setup_inputs(seed: int = 0) -> dict:
    splits = jax.random.split(jax.random.key(seed), 3)
    voltages = touch_ends(jax.random.randint(splits[0], (N_IN, SPECTRA, 2, NCHAN), -127, 128), jax.random.fold_in(splits[0], 1), -127, 127).astype(jnp.int32)
    tile_map = jax.random.permutation(splits[1], NTILES).astype(jnp.int32)
    return {"voltages": voltages, "tile_map": tile_map}


def filter_table(channels, first_channel):
    sample_idx = jnp.arange(TAPS * NCHAN, dtype=jnp.int32)
    position = (sample_idx.astype(jnp.float32) + 0.5) / NCHAN - TAPS / 2.0
    hann_taper = 0.5 - 0.5 * jnp.cos((sample_idx.astype(jnp.float32) + 0.5) * (2.0 * math.pi / (TAPS * NCHAN)))
    prototype = (jnp.sinc(position) * hann_taper / (128.0 * math.sqrt(NCHAN))).reshape(TAPS, NCHAN)
    sample_col = jnp.arange(NCHAN, dtype=jnp.int32)
    channel_row = first_channel + jnp.arange(channels, dtype=jnp.int32)
    phase_index = sample_col[:, None] * channel_row[None, :] % NCHAN
    angles = phase_index.astype(jnp.float32) * (2.0 * math.pi / NCHAN)
    cosine = jnp.cos(angles)
    sine_part = jnp.sin(angles)
    upper = jnp.stack([cosine, -sine_part], axis=-1)
    lower = jnp.stack([sine_part, cosine], axis=-1)
    pattern = jnp.stack([upper, lower], axis=0)
    table = prototype[:, None, :, None, None] * pattern[None]
    return table.astype(jnp.bfloat16).reshape(TAPS, 2 * NCHAN, 2 * channels)

def tile_coords(tile_id, blocks):
    step_row = jnp.arange(1, blocks, dtype=jnp.int32)
    triangle = step_row * (step_row + 1) // 2
    row_block = lax.optimization_barrier(jnp.sum((tile_id[..., None] >= triangle).astype(jnp.int32), axis=-1))
    col_block = tile_id - row_block * (row_block + 1) // 2
    return (row_block.astype(jnp.int32), col_block.astype(jnp.int32))

def reference(voltages, tile_map):
    filters = filter_table(CHANNELS, FIRST)
    grouped = voltages.reshape(N_IN // 16, 16, SPECTRA, 2 * NCHAN)

    def channelize(input_group):
        samples = input_group.astype(jnp.bfloat16)
        extended = jnp.concatenate([jnp.zeros((16, TAPS - 1, 2 * NCHAN), jnp.bfloat16), samples], axis=1)
        accum_sum = jnp.zeros((16 * SPECTRA, 2 * CHANNELS), jnp.float32)
        for tap_index in range(TAPS):
            window = extended[:, tap_index:tap_index + SPECTRA].reshape(16 * SPECTRA, 2 * NCHAN)
            accum_sum = accum_sum + jnp.dot(window, filters[tap_index], preferred_element_type=jnp.float32)
        return accum_sum.astype(jnp.bfloat16)
    spectra = lax.map(channelize, grouped)
    spectra = spectra.reshape(N_IN, SPECTRA, CHANNELS, 2).transpose(2, 3, 1, 0)

    def one_tile(tile_id):
        row_block, col_block = tile_coords(tile_id, N_IN // TB)
        row_tiles = lax.dynamic_slice_in_dim(spectra, row_block * TB, TB, 3).astype(jnp.float32)
        col_tiles = lax.dynamic_slice_in_dim(spectra, col_block * TB, TB, 3).astype(jnp.float32)
        turned = jnp.stack([row_tiles[:, 1], -row_tiles[:, 0]], axis=1)
        paired = jnp.stack([row_tiles, turned], axis=1)
        products = jnp.einsum('hqptx,hpty->hqxy', paired, col_tiles, precision=lax.Precision.HIGHEST)
        return products * (1.0 / SPECTRA)
    return lax.map(one_tile, tile_map)
```

```python
import math

import jax
import jax.numpy as jnp
from jax import lax
from jax.experimental import pallas as pl
from jax.experimental.pallas import tpu as pltpu
from jax.sharding import PartitionSpec as P

NCHAN = 4096
TAPS = 4
TB = 128
CH_DEV = 2
C_BLOCK = 512


def passed_along(value, axis, steps):
    count = lax.axis_size(axis)
    leading, last = (max(0, -steps), min(count, count - steps))
    return lax.ppermute(value, axis, [(source, source + steps) for source in range(leading, last)])


def prototype_rows():
    sample_idx = jnp.arange(TAPS * NCHAN, dtype=jnp.int32)
    position = (sample_idx.astype(jnp.float32) + 0.5) / NCHAN - TAPS / 2.0
    hann_taper = 0.5 - 0.5 * jnp.cos(
        (sample_idx.astype(jnp.float32) + 0.5) * (2.0 * math.pi / (TAPS * NCHAN))
    )
    return (jnp.sinc(position) * hann_taper / (128.0 * math.sqrt(NCHAN))).reshape(TAPS, NCHAN)


def channelize_kernel(first_channel, channels, proto_ref, x_ref, out_ref, acc_ref):
    step = pl.program_id(0)
    cb = x_ref.shape[-1]
    width = 2 * channels
    lane = lax.broadcasted_iota(jnp.int32, (cb, width), 1)
    sample = lax.broadcasted_iota(jnp.int32, (cb, width), 0) + step * cb
    upper = lane >= channels
    channel = first_channel + jnp.where(upper, lane - channels, lane)
    phase = (sample * channel) % NCHAN
    phase = jnp.where(upper, (phase + NCHAN // 4) % NCHAN, phase)
    cos_part = jnp.cos(phase.astype(jnp.float32) * (2.0 * math.pi / NCHAN))
    sin_part = pltpu.roll(cos_part, channels, 1) * jnp.where(upper, 1.0, -1.0).astype(jnp.float32)
    weights = proto_ref[...]
    re_tables = []
    im_tables = []
    for tap in range(TAPS):
        w = weights[:, tap : tap + 1]
        re_tables.append((w * cos_part).astype(jnp.bfloat16))
        im_tables.append((w * sin_part).astype(jnp.bfloat16))
    re_table = jnp.concatenate(re_tables, axis=1)
    im_table = jnp.concatenate(im_tables, axis=1)
    rows = x_ref.shape[0] * x_ref.shape[1]
    x_re = x_ref[:, :, 0, :].reshape(rows, cb).astype(jnp.bfloat16)
    x_im = x_ref[:, :, 1, :].reshape(rows, cb).astype(jnp.bfloat16)
    part = jnp.dot(x_re, re_table, preferred_element_type=jnp.float32) + jnp.dot(
        x_im, im_table, preferred_element_type=jnp.float32
    )

    @pl.when(step == 0)
    def _():
        acc_ref[...] = part

    @pl.when(step > 0)
    def _():
        acc_ref[...] += part

    @pl.when(step == pl.num_programs(0) - 1)
    def _():
        out_ref[...] = acc_ref[...]


def tap_products(voltages, proto_t, first_channel, channels):
    local_inputs, time_steps = voltages.shape[0], voltages.shape[1]
    rows = local_inputs * time_steps
    width = TAPS * 2 * channels
    blocks = NCHAN // C_BLOCK
    kernel = lambda *refs: channelize_kernel(first_channel, channels, *refs)
    return pl.pallas_call(
        kernel,
        out_shape=jax.ShapeDtypeStruct((rows, width), jnp.float32),
        grid=(blocks,),
        in_specs=[
            pl.BlockSpec((C_BLOCK, TAPS), lambda j: (j, 0)),
            pl.BlockSpec((local_inputs, time_steps, 2, C_BLOCK), lambda j: (0, 0, 0, j)),
        ],
        out_specs=pl.BlockSpec((rows, width), lambda j: (0, 0)),
        scratch_shapes=[pltpu.VMEM((rows, width), jnp.float32)],
        compiler_params=pltpu.CompilerParams(
            dimension_semantics=("arbitrary",), vmem_limit_bytes=48 * 1024 * 1024
        ),
        cost_estimate=pl.CostEstimate(
            flops=2 * rows * 2 * NCHAN * width,
            transcendentals=NCHAN * 2 * channels,
            bytes_accessed=voltages.size * 4 + rows * width * 4,
        ),
    )(proto_t, voltages)


def tile_coords(tile_id, blocks):
    step_row = jnp.arange(1, blocks, dtype=jnp.int32)
    triangle = step_row * (step_row + 1) // 2
    row_block = jnp.sum((tile_id[..., None] >= triangle).astype(jnp.int32), axis=-1)
    col_block = tile_id - row_block * (row_block + 1) // 2
    return (row_block, col_block)


def arrange_rows(gathered, time_steps):
    piece_count = gathered.shape[0]
    freq_count = gathered.shape[1]
    local_chans = gathered.shape[2]
    inner_width = gathered.shape[4] // time_steps
    unfolded = gathered.reshape(piece_count, freq_count, local_chans, 2, time_steps, inner_width)
    unfolded = unfolded.transpose(2, 3, 0, 4, 1, 5)
    return unfolded.reshape(local_chans, 2, piece_count * time_steps, freq_count * inner_width)


def tile_products(spectra, tile_ids):
    blocks = spectra.shape[3] // TB
    row_block, col_block = tile_coords(tile_ids, blocks)
    shaped = spectra.reshape(spectra.shape[0], 2, spectra.shape[2], blocks, TB)
    row_tiles = jnp.take(shaped, row_block, axis=3)
    col_tiles = jnp.take(shaped, col_block, axis=3)
    turned = jnp.stack([row_tiles[:, 1], -row_tiles[:, 0]], axis=1)
    paired = jnp.stack([row_tiles, turned], axis=1)
    return jnp.einsum("hqptsx,hptsy->shqxy", paired, col_tiles, preferred_element_type=jnp.float32)


def on_device(voltages, tile_map):
    local_inputs = voltages.shape[0]
    time_steps = voltages.shape[1]
    freq_devices = lax.axis_size("freq")
    time_devices = lax.axis_size("tm")
    channels = CH_DEV * freq_devices
    first_channel = NCHAN // 2 - channels // 2
    proto_t = prototype_rows().T
    products = tap_products(voltages, proto_t, first_channel, channels)
    products = products.reshape(local_inputs, time_steps, TAPS, 2, channels)
    tail = products[:, time_steps - (TAPS - 1) :]
    if time_devices > 1:
        previous = passed_along(tail, "tm", 1)
    else:
        previous = jnp.zeros_like(tail)
    total = None
    for tap in range(TAPS):
        lead = TAPS - 1 - tap
        shifted = jnp.concatenate(
            [previous[:, tap:, tap], products[:, : time_steps - lead, tap]], axis=1
        )
        total = shifted if total is None else total + shifted
    spectra = total.astype(jnp.bfloat16)
    spectra = spectra.reshape(local_inputs, time_steps, 2, freq_devices, CH_DEV)
    spectra = spectra.transpose(3, 4, 2, 1, 0).reshape(
        freq_devices, CH_DEV, 2, time_steps * local_inputs
    )
    turned = lax.all_to_all(spectra, "freq", split_axis=0, concat_axis=0, tiled=True)
    slot_count = tile_map.shape[0] // time_devices
    inverse_count = 1.0 / (time_steps * time_devices)
    tile_ids = lax.dynamic_slice_in_dim(tile_map, lax.axis_index("tm") * slot_count, slot_count)
    summed = tile_products(
        arrange_rows(lax.all_gather(turned[None], "tm", axis=0, tiled=True), time_steps), tile_ids
    )
    return summed * inverse_count


def solution(mesh):
    in_specs = (P("freq", "tm", None, None), P())
    out_specs = P("tm", "freq", None, None, None)
    return jax.shard_map(
        on_device, mesh=mesh, in_specs=in_specs, out_specs=out_specs, check_vma=False
    )
```

```python
import math

import jax
import jax.numpy as jnp
from jax import lax
from jax.experimental import pallas as pl
from jax.experimental.pallas import tpu as pltpu
from jax.sharding import PartitionSpec as P

NCHAN = 4096
TAPS = 4
TB = 128
CH_DEV = 2
C_BLOCK = 512


def passed_along(value, axis, steps):
    count = lax.axis_size(axis)
    leading, last = (max(0, -steps), min(count, count - steps))
    return lax.ppermute(value, axis, [(source, source + steps) for source in range(leading, last)])


def prototype_rows():
    sample_idx = jnp.arange(TAPS * NCHAN, dtype=jnp.int32)
    position = (sample_idx.astype(jnp.float32) + 0.5) / NCHAN - TAPS / 2.0
    hann_taper = 0.5 - 0.5 * jnp.cos(
        (sample_idx.astype(jnp.float32) + 0.5) * (2.0 * math.pi / (TAPS * NCHAN))
    )
    return (jnp.sinc(position) * hann_taper / (128.0 * math.sqrt(NCHAN))).reshape(TAPS, NCHAN)


def phase_table(first_channel, channels):
    radix = 64
    channel = first_channel + jnp.arange(channels, dtype=jnp.int32)
    digit = jnp.arange(radix, dtype=jnp.int32)
    step = 2.0 * math.pi / NCHAN
    high = ((digit[None, :] * radix * channel[:, None]) % NCHAN).astype(jnp.float32) * step
    low = ((digit[None, :] * channel[:, None]) % NCHAN).astype(jnp.float32) * step
    cos_hi, sin_hi = jnp.cos(high)[:, :, None], jnp.sin(high)[:, :, None]
    cos_lo, sin_lo = jnp.cos(low)[:, None, :], jnp.sin(low)[:, None, :]
    cosine = (cos_hi * cos_lo - sin_hi * sin_lo).reshape(channels, NCHAN)
    sine = (sin_hi * cos_lo + cos_hi * sin_lo).reshape(channels, NCHAN)
    return jnp.concatenate([cosine, -sine], axis=0)


def channelize_kernel(channels, proto_ref, phase_ref, x_ref, out_ref, acc_ref):
    step = pl.program_id(0)
    cb = x_ref.shape[-1]
    upper = phase_ref[...]
    lower = jnp.concatenate([-upper[channels:], upper[:channels]], axis=0)
    weights = proto_ref[...]
    re_tables = []
    im_tables = []
    for tap in range(TAPS):
        w = weights[tap : tap + 1, :]
        re_tables.append((w * upper).astype(jnp.bfloat16))
        im_tables.append((w * lower).astype(jnp.bfloat16))
    re_table = jnp.concatenate(re_tables, axis=0)
    im_table = jnp.concatenate(im_tables, axis=0)
    rows = x_ref.shape[0] * x_ref.shape[1]
    x_re = x_ref[:, :, 0, :].reshape(rows, cb).astype(jnp.bfloat16)
    x_im = x_ref[:, :, 1, :].reshape(rows, cb).astype(jnp.bfloat16)
    dims = (((1,), (1,)), ((), ()))
    part = lax.dot_general(x_re, re_table, dims, preferred_element_type=jnp.float32) + lax.dot_general(
        x_im, im_table, dims, preferred_element_type=jnp.float32
    )

    @pl.when(step == 0)
    def _():
        acc_ref[...] = part

    @pl.when(step > 0)
    def _():
        acc_ref[...] += part

    @pl.when(step == pl.num_programs(0) - 1)
    def _():
        out_ref[...] = acc_ref[...]


def tap_products(voltages, proto, phase, channels):
    local_inputs, time_steps = voltages.shape[0], voltages.shape[1]
    rows = local_inputs * time_steps
    width = TAPS * 2 * channels
    blocks = NCHAN // C_BLOCK
    kernel = lambda *refs: channelize_kernel(channels, *refs)
    return pl.pallas_call(
        kernel,
        out_shape=jax.ShapeDtypeStruct((rows, width), jnp.float32),
        grid=(blocks,),
        in_specs=[
            pl.BlockSpec((TAPS, C_BLOCK), lambda j: (0, j)),
            pl.BlockSpec((2 * channels, C_BLOCK), lambda j: (0, j)),
            pl.BlockSpec((local_inputs, time_steps, 2, C_BLOCK), lambda j: (0, 0, 0, j)),
        ],
        out_specs=pl.BlockSpec((rows, width), lambda j: (0, 0)),
        scratch_shapes=[pltpu.VMEM((rows, width), jnp.float32)],
        compiler_params=pltpu.CompilerParams(
            dimension_semantics=("arbitrary",), vmem_limit_bytes=48 * 1024 * 1024
        ),
        cost_estimate=pl.CostEstimate(
            flops=2 * rows * 2 * NCHAN * width,
            transcendentals=0,
            bytes_accessed=voltages.size * 4 + rows * width * 4 + phase.size * 4,
        ),
    )(proto, phase, voltages)


def tile_coords(tile_id, blocks):
    step_row = jnp.arange(1, blocks, dtype=jnp.int32)
    triangle = step_row * (step_row + 1) // 2
    row_block = jnp.sum((tile_id[..., None] >= triangle).astype(jnp.int32), axis=-1)
    col_block = tile_id - row_block * (row_block + 1) // 2
    return (row_block, col_block)


def arrange_rows(gathered, time_steps):
    piece_count = gathered.shape[0]
    freq_count = gathered.shape[1]
    local_chans = gathered.shape[2]
    inner_width = gathered.shape[4] // time_steps
    unfolded = gathered.reshape(piece_count, freq_count, local_chans, 2, time_steps, inner_width)
    unfolded = unfolded.transpose(2, 3, 0, 4, 1, 5)
    return unfolded.reshape(local_chans, 2, piece_count * time_steps, freq_count * inner_width)


def tile_products(spectra, tile_ids):
    blocks = spectra.shape[3] // TB
    row_block, col_block = tile_coords(tile_ids, blocks)
    shaped = spectra.reshape(spectra.shape[0], 2, spectra.shape[2], blocks, TB)
    row_tiles = jnp.take(shaped, row_block, axis=3)
    col_tiles = jnp.take(shaped, col_block, axis=3)
    turned = jnp.stack([row_tiles[:, 1], -row_tiles[:, 0]], axis=1)
    paired = jnp.stack([row_tiles, turned], axis=1)
    return jnp.einsum("hqptsx,hptsy->shqxy", paired, col_tiles, preferred_element_type=jnp.float32)


def on_device(voltages, tile_map):
    local_inputs = voltages.shape[0]
    time_steps = voltages.shape[1]
    freq_devices = lax.axis_size("freq")
    time_devices = lax.axis_size("tm")
    channels = CH_DEV * freq_devices
    first_channel = NCHAN // 2 - channels // 2
    proto = prototype_rows()
    phase = phase_table(first_channel, channels)
    products = tap_products(voltages, proto, phase, channels)
    products = products.reshape(local_inputs, time_steps, TAPS, 2, channels)
    tail = products[:, time_steps - (TAPS - 1) :]
    if time_devices > 1:
        previous = passed_along(tail, "tm", 1)
    else:
        previous = jnp.zeros_like(tail)
    total = None
    for tap in range(TAPS):
        lead = TAPS - 1 - tap
        shifted = jnp.concatenate(
            [previous[:, tap:, tap], products[:, : time_steps - lead, tap]], axis=1
        )
        total = shifted if total is None else total + shifted
    spectra = total.astype(jnp.bfloat16)
    spectra = spectra.reshape(local_inputs, time_steps, 2, freq_devices, CH_DEV)
    spectra = spectra.transpose(3, 4, 2, 1, 0).reshape(
        freq_devices, CH_DEV, 2, time_steps * local_inputs
    )
    turned = lax.all_to_all(spectra, "freq", split_axis=0, concat_axis=0, tiled=True)
    slot_count = tile_map.shape[0] // time_devices
    inverse_count = 1.0 / (time_steps * time_devices)
    tile_ids = lax.dynamic_slice_in_dim(tile_map, lax.axis_index("tm") * slot_count, slot_count)
    summed = tile_products(
        arrange_rows(lax.all_gather(turned[None], "tm", axis=0, tiled=True), time_steps), tile_ids
    )
    return summed * inverse_count


def solution(mesh):
    in_specs = (P("freq", "tm", None, None), P())
    out_specs = P("tm", "freq", None, None, None)
    return jax.shard_map(
        on_device, mesh=mesh, in_specs=in_specs, out_specs=out_specs, check_vma=False
    )
```

```python
import math

import jax
import jax.numpy as jnp
from jax import lax
from jax.experimental import pallas as pl
from jax.experimental.pallas import tpu as pltpu
from jax.sharding import PartitionSpec as P

NCHAN = 4096
TAPS = 4
TB = 128
CH_DEV = 2
C_BLOCK = 512


def passed_along(value, axis, steps):
    count = lax.axis_size(axis)
    leading, last = (max(0, -steps), min(count, count - steps))
    return lax.ppermute(value, axis, [(source, source + steps) for source in range(leading, last)])


def prototype_rows():
    sample_idx = jnp.arange(TAPS * NCHAN, dtype=jnp.int32)
    position = (sample_idx.astype(jnp.float32) + 0.5) / NCHAN - TAPS / 2.0
    hann_taper = 0.5 - 0.5 * jnp.cos(
        (sample_idx.astype(jnp.float32) + 0.5) * (2.0 * math.pi / (TAPS * NCHAN))
    )
    return (jnp.sinc(position) * hann_taper / (128.0 * math.sqrt(NCHAN))).reshape(TAPS, NCHAN)


def phase_tables(first_channel, channels):
    channel = first_channel + jnp.arange(channels, dtype=jnp.int32)
    step = 2.0 * math.pi / NCHAN
    lane = jnp.arange(C_BLOCK, dtype=jnp.int32)
    start = ((lane[None, :] * channel[:, None]) % NCHAN).astype(jnp.float32) * step
    first = jnp.concatenate([jnp.cos(start), jnp.sin(start)], axis=0)
    block = jnp.arange(NCHAN // C_BLOCK, dtype=jnp.int32) * C_BLOCK
    shift = ((block[:, None] * channel[None, :]) % NCHAN).astype(jnp.float32) * step
    turn = jnp.concatenate([jnp.cos(shift), jnp.sin(shift)], axis=1)
    return first, jnp.broadcast_to(turn[:, :, None], turn.shape + (128,))


def channelize_kernel(channels, proto_ref, first_ref, turn_ref, x_hbm, out_ref, buf, sems, acc_ref):
    step = pl.program_id(0)
    count = pl.num_programs(0)
    cb = buf.shape[-1]

    def fetch(block, slot):
        for part in range(2):
            pltpu.make_async_copy(
                x_hbm.at[:, :, part, pl.ds(block * cb, cb)], buf.at[slot, part], sems.at[slot, part]
            ).start()

    @pl.when(step == 0)
    def _():
        fetch(0, 0)

    @pl.when(step + 1 < count)
    def _():
        fetch(step + 1, (step + 1) % 2)

    slot = step % 2
    for part in range(2):
        pltpu.make_async_copy(
            x_hbm.at[:, :, part, pl.ds(0, cb)], buf.at[slot, part], sems.at[slot, part]
        ).wait()
    turn = jnp.concatenate([turn_ref[...]] * (cb // turn_ref.shape[-1]), axis=1)
    cos_0, sin_0 = first_ref[:channels], first_ref[channels:]
    cos_t, sin_t = turn[:channels], turn[channels:]
    cosine = cos_0 * cos_t - sin_0 * sin_t
    sine = sin_0 * cos_t + cos_0 * sin_t
    upper = jnp.concatenate([cosine, -sine], axis=0)
    lower = jnp.concatenate([sine, cosine], axis=0)
    weights = proto_ref[...]
    re_tables = []
    im_tables = []
    for tap in range(TAPS):
        w = weights[tap : tap + 1, :]
        re_tables.append((w * upper).astype(jnp.bfloat16))
        im_tables.append((w * lower).astype(jnp.bfloat16))
    re_table = jnp.concatenate(re_tables, axis=0)
    im_table = jnp.concatenate(im_tables, axis=0)
    rows = buf.shape[2] * buf.shape[3]
    x_re = buf[slot, 0].reshape(rows, cb).astype(jnp.bfloat16)
    x_im = buf[slot, 1].reshape(rows, cb).astype(jnp.bfloat16)
    dims = (((1,), (1,)), ((), ()))
    part = lax.dot_general(x_re, re_table, dims, preferred_element_type=jnp.float32) + lax.dot_general(
        x_im, im_table, dims, preferred_element_type=jnp.float32
    )

    @pl.when(step == 0)
    def _():
        acc_ref[...] = part

    @pl.when(step > 0)
    def _():
        acc_ref[...] += part

    @pl.when(step == pl.num_programs(0) - 1)
    def _():
        out_ref[...] = acc_ref[...]


def tap_products(voltages, proto, first, turn, channels):
    local_inputs, time_steps = voltages.shape[0], voltages.shape[1]
    rows = local_inputs * time_steps
    width = TAPS * 2 * channels
    blocks = NCHAN // C_BLOCK
    kernel = lambda *refs: channelize_kernel(channels, *refs)
    return pl.pallas_call(
        kernel,
        out_shape=jax.ShapeDtypeStruct((rows, width), jnp.float32),
        grid=(blocks,),
        in_specs=[
            pl.BlockSpec((TAPS, C_BLOCK), lambda j: (0, j)),
            pl.BlockSpec((2 * channels, C_BLOCK), lambda j: (0, 0)),
            pl.BlockSpec((None, 2 * channels, 128), lambda j: (j, 0, 0)),
            pl.BlockSpec(memory_space=pl.ANY),
        ],
        out_specs=pl.BlockSpec((rows, width), lambda j: (0, 0)),
        scratch_shapes=[
            pltpu.VMEM((2, 2, local_inputs, time_steps, C_BLOCK), jnp.int32),
            pltpu.SemaphoreType.DMA((2, 2)),
            pltpu.VMEM((rows, width), jnp.float32),
        ],
        compiler_params=pltpu.CompilerParams(
            dimension_semantics=("arbitrary",), vmem_limit_bytes=48 * 1024 * 1024
        ),
        cost_estimate=pl.CostEstimate(
            flops=2 * rows * 2 * NCHAN * width,
            transcendentals=0,
            bytes_accessed=voltages.size * 4 + rows * width * 4 + first.size * 4 + turn.size * 4,
        ),
    )(proto, first, turn, voltages)


def tile_coords(tile_id, blocks):
    step_row = jnp.arange(1, blocks, dtype=jnp.int32)
    triangle = step_row * (step_row + 1) // 2
    row_block = jnp.sum((tile_id[..., None] >= triangle).astype(jnp.int32), axis=-1)
    col_block = tile_id - row_block * (row_block + 1) // 2
    return (row_block, col_block)


def arrange_rows(gathered, time_steps):
    piece_count = gathered.shape[0]
    freq_count = gathered.shape[1]
    local_chans = gathered.shape[2]
    inner_width = gathered.shape[4] // time_steps
    unfolded = gathered.reshape(piece_count, freq_count, local_chans, 2, time_steps, inner_width)
    unfolded = unfolded.transpose(2, 3, 0, 4, 1, 5)
    return unfolded.reshape(local_chans, 2, piece_count * time_steps, freq_count * inner_width)


def tile_products(spectra, tile_ids):
    blocks = spectra.shape[3] // TB
    row_block, col_block = tile_coords(tile_ids, blocks)
    shaped = spectra.reshape(spectra.shape[0], 2, spectra.shape[2], blocks, TB)
    row_tiles = jnp.take(shaped, row_block, axis=3)
    col_tiles = jnp.take(shaped, col_block, axis=3)
    turned = jnp.stack([row_tiles[:, 1], -row_tiles[:, 0]], axis=1)
    paired = jnp.stack([row_tiles, turned], axis=1)
    return jnp.einsum("hqptsx,hptsy->shqxy", paired, col_tiles, preferred_element_type=jnp.float32)


def on_device(voltages, tile_map):
    local_inputs = voltages.shape[0]
    time_steps = voltages.shape[1]
    freq_devices = lax.axis_size("freq")
    time_devices = lax.axis_size("tm")
    channels = CH_DEV * freq_devices
    first_channel = NCHAN // 2 - channels // 2
    proto = prototype_rows()
    first, turn = phase_tables(first_channel, channels)
    products = tap_products(voltages, proto, first, turn, channels)
    products = products.reshape(local_inputs, time_steps, TAPS, 2, channels)
    tail = products[:, time_steps - (TAPS - 1) :]
    if time_devices > 1:
        previous = passed_along(tail, "tm", 1)
    else:
        previous = jnp.zeros_like(tail)
    total = None
    for tap in range(TAPS):
        lead = TAPS - 1 - tap
        shifted = jnp.concatenate(
            [previous[:, tap:, tap], products[:, : time_steps - lead, tap]], axis=1
        )
        total = shifted if total is None else total + shifted
    spectra = total.astype(jnp.bfloat16)
    spectra = spectra.reshape(local_inputs, time_steps, 2, freq_devices, CH_DEV)
    spectra = spectra.transpose(3, 4, 2, 1, 0).reshape(
        freq_devices, CH_DEV, 2, time_steps * local_inputs
    )
    turned = lax.all_to_all(spectra, "freq", split_axis=0, concat_axis=0, tiled=True)
    slot_count = tile_map.shape[0] // time_devices
    inverse_count = 1.0 / (time_steps * time_devices)
    tile_ids = lax.dynamic_slice_in_dim(tile_map, lax.axis_index("tm") * slot_count, slot_count)
    summed = tile_products(
        arrange_rows(lax.all_gather(turned[None], "tm", axis=0, tiled=True), time_steps), tile_ids
    )
    return summed * inverse_count


def solution(mesh):
    in_specs = (P("freq", "tm", None, None), P())
    out_specs = P("tm", "freq", None, None, None)
    return jax.shard_map(
        on_device, mesh=mesh, in_specs=in_specs, out_specs=out_specs, check_vma=False
    )
```

```python
import math

import jax
import jax.numpy as jnp
from jax import lax
from jax.experimental import pallas as pl
from jax.experimental.pallas import tpu as pltpu
from jax.sharding import PartitionSpec as P

NCHAN = 4096
TAPS = 4
TB = 128
CH_DEV = 2
C_BLOCK = 512


def passed_along(value, axis, steps):
    count = lax.axis_size(axis)
    leading, last = (max(0, -steps), min(count, count - steps))
    return lax.ppermute(value, axis, [(source, source + steps) for source in range(leading, last)])


def prototype_rows():
    sample_idx = jnp.arange(TAPS * NCHAN, dtype=jnp.int32)
    position = (sample_idx.astype(jnp.float32) + 0.5) / NCHAN - TAPS / 2.0
    hann_taper = 0.5 - 0.5 * jnp.cos(
        (sample_idx.astype(jnp.float32) + 0.5) * (2.0 * math.pi / (TAPS * NCHAN))
    )
    return (jnp.sinc(position) * hann_taper / (128.0 * math.sqrt(NCHAN))).reshape(TAPS, NCHAN)


def phase_tables(first_channel, channels):
    channel = first_channel + jnp.arange(channels, dtype=jnp.int32)
    step = 2.0 * math.pi / NCHAN
    lane = jnp.arange(C_BLOCK, dtype=jnp.int32)
    start = ((lane[None, :] * channel[:, None]) % NCHAN).astype(jnp.float32) * step
    first = jnp.concatenate([jnp.cos(start), jnp.sin(start)], axis=0)
    block = jnp.arange(NCHAN // C_BLOCK, dtype=jnp.int32) * C_BLOCK
    shift = ((block[:, None] * channel[None, :]) % NCHAN).astype(jnp.float32) * step
    turn = jnp.concatenate([jnp.cos(shift), jnp.sin(shift)], axis=1)
    return first, jnp.broadcast_to(turn[:, :, None], turn.shape + (128,))


def channelize_kernel(
    channels, fold_shift, proto_ref, first_ref, turn_ref, x_hbm, out_ref, buf, sems, acc_ref
):
    step = pl.program_id(0)
    count = pl.num_programs(0)
    cb = buf.shape[-1]

    def fetch(block, slot):
        for part in range(2):
            pltpu.make_async_copy(
                x_hbm.at[:, :, part, pl.ds(block * cb, cb)], buf.at[slot, part], sems.at[slot, part]
            ).start()

    @pl.when(step == 0)
    def _():
        fetch(0, 0)

    @pl.when(step + 1 < count)
    def _():
        fetch(step + 1, (step + 1) % 2)

    slot = step % 2
    for part in range(2):
        pltpu.make_async_copy(
            x_hbm.at[:, :, part, pl.ds(0, cb)], buf.at[slot, part], sems.at[slot, part]
        ).wait()
    turn = jnp.concatenate([turn_ref[...]] * (cb // turn_ref.shape[-1]), axis=1)
    cos_0, sin_0 = first_ref[:channels], first_ref[channels:]
    cos_t, sin_t = turn[:channels], turn[channels:]
    cosine = cos_0 * cos_t - sin_0 * sin_t
    sine = sin_0 * cos_t + cos_0 * sin_t
    upper = jnp.concatenate([cosine, -sine], axis=0)
    lower = jnp.concatenate([sine, cosine], axis=0)
    weights = proto_ref[...]
    re_tables = []
    im_tables = []
    for tap in range(TAPS):
        w = weights[tap : tap + 1, :]
        re_tables.append((w * upper).astype(jnp.bfloat16))
        im_tables.append((w * lower).astype(jnp.bfloat16))
    re_table = jnp.concatenate(re_tables, axis=0)
    im_table = jnp.concatenate(im_tables, axis=0)
    rows = buf.shape[2] * buf.shape[3]
    x_re = buf[slot, 0].reshape(rows, cb).astype(jnp.bfloat16)
    x_im = buf[slot, 1].reshape(rows, cb).astype(jnp.bfloat16)
    dims = (((1,), (1,)), ((), ()))
    part = lax.dot_general(x_re, re_table, dims, preferred_element_type=jnp.float32) + lax.dot_general(
        x_im, im_table, dims, preferred_element_type=jnp.float32
    )

    @pl.when(step == 0)
    def _():
        acc_ref[...] = part

    @pl.when(jnp.logical_and(step > 0, step < count - 1))
    def _():
        acc_ref[...] += part

    @pl.when(step == count - 1)
    def _():
        products = acc_ref[...] + part
        if not fold_shift:
            out_ref[...] = products
            return
        time_steps = buf.shape[3]
        width = 2 * channels
        block = lax.broadcasted_iota(jnp.int32, (rows, width), 0) % time_steps
        total = None
        for tap in range(TAPS):
            term = products[:, tap * width : (tap + 1) * width]
            lead = TAPS - 1 - tap
            if lead:
                term = jnp.where(block >= lead, pltpu.roll(term, lead, 0), 0.0)
            total = term if total is None else total + term
        out_ref[...] = total.astype(out_ref.dtype)


def tap_products(voltages, proto, first, turn, channels, fold_shift):
    local_inputs, time_steps = voltages.shape[0], voltages.shape[1]
    rows = local_inputs * time_steps
    width = TAPS * 2 * channels
    blocks = NCHAN // C_BLOCK
    kernel = lambda *refs: channelize_kernel(channels, fold_shift, *refs)
    if fold_shift:
        out_shape = jax.ShapeDtypeStruct((rows, 2 * channels), jnp.bfloat16)
    else:
        out_shape = jax.ShapeDtypeStruct((rows, width), jnp.float32)
    return pl.pallas_call(
        kernel,
        out_shape=out_shape,
        grid=(blocks,),
        in_specs=[
            pl.BlockSpec((TAPS, C_BLOCK), lambda j: (0, j)),
            pl.BlockSpec((2 * channels, C_BLOCK), lambda j: (0, 0)),
            pl.BlockSpec((None, 2 * channels, 128), lambda j: (j, 0, 0)),
            pl.BlockSpec(memory_space=pl.ANY),
        ],
        out_specs=pl.BlockSpec(out_shape.shape, lambda j: (0, 0)),
        scratch_shapes=[
            pltpu.VMEM((2, 2, local_inputs, time_steps, C_BLOCK), jnp.int32),
            pltpu.SemaphoreType.DMA((2, 2)),
            pltpu.VMEM((rows, width), jnp.float32),
        ],
        compiler_params=pltpu.CompilerParams(
            dimension_semantics=("arbitrary",), vmem_limit_bytes=48 * 1024 * 1024
        ),
        cost_estimate=pl.CostEstimate(
            flops=2 * rows * 2 * NCHAN * width,
            transcendentals=0,
            bytes_accessed=voltages.size * 4 + rows * width * 4 + first.size * 4 + turn.size * 4,
        ),
    )(proto, first, turn, voltages)


def tile_coords(tile_id, blocks):
    step_row = jnp.arange(1, blocks, dtype=jnp.int32)
    triangle = step_row * (step_row + 1) // 2
    row_block = jnp.sum((tile_id[..., None] >= triangle).astype(jnp.int32), axis=-1)
    col_block = tile_id - row_block * (row_block + 1) // 2
    return (row_block, col_block)


def arrange_rows(gathered, time_steps):
    piece_count = gathered.shape[0]
    freq_count = gathered.shape[1]
    local_chans = gathered.shape[2]
    inner_width = gathered.shape[4] // time_steps
    unfolded = gathered.reshape(piece_count, freq_count, local_chans, 2, time_steps, inner_width)
    unfolded = unfolded.transpose(2, 3, 0, 4, 1, 5)
    return unfolded.reshape(local_chans, 2, piece_count * time_steps, freq_count * inner_width)


def tile_products(spectra, tile_ids):
    blocks = spectra.shape[3] // TB
    row_block, col_block = tile_coords(tile_ids, blocks)
    shaped = spectra.reshape(spectra.shape[0], 2, spectra.shape[2], blocks, TB)
    row_tiles = jnp.take(shaped, row_block, axis=3)
    col_tiles = jnp.take(shaped, col_block, axis=3)
    turned = jnp.stack([row_tiles[:, 1], -row_tiles[:, 0]], axis=1)
    paired = jnp.stack([row_tiles, turned], axis=1)
    return jnp.einsum("hqptsx,hptsy->shqxy", paired, col_tiles, preferred_element_type=jnp.float32)


def on_device(voltages, tile_map):
    local_inputs = voltages.shape[0]
    time_steps = voltages.shape[1]
    freq_devices = lax.axis_size("freq")
    time_devices = lax.axis_size("tm")
    channels = CH_DEV * freq_devices
    first_channel = NCHAN // 2 - channels // 2
    proto = prototype_rows()
    first, turn = phase_tables(first_channel, channels)
    if time_devices == 1:
        spectra = tap_products(voltages, proto, first, turn, channels, True)
    else:
        products = tap_products(voltages, proto, first, turn, channels, False)
        products = products.reshape(local_inputs, time_steps, TAPS, 2, channels)
        tail = products[:, time_steps - (TAPS - 1) :]
        previous = passed_along(tail, "tm", 1)
        total = None
        for tap in range(TAPS):
            lead = TAPS - 1 - tap
            shifted = jnp.concatenate(
                [previous[:, tap:, tap], products[:, : time_steps - lead, tap]], axis=1
            )
            total = shifted if total is None else total + shifted
        spectra = total.astype(jnp.bfloat16)
    spectra = spectra.reshape(local_inputs, time_steps, 2, freq_devices, CH_DEV)
    spectra = spectra.transpose(3, 4, 2, 1, 0).reshape(
        freq_devices, CH_DEV, 2, time_steps * local_inputs
    )
    turned = lax.all_to_all(spectra, "freq", split_axis=0, concat_axis=0, tiled=True)
    slot_count = tile_map.shape[0] // time_devices
    inverse_count = 1.0 / (time_steps * time_devices)
    tile_ids = lax.dynamic_slice_in_dim(tile_map, lax.axis_index("tm") * slot_count, slot_count)
    summed = tile_products(
        arrange_rows(lax.all_gather(turned[None], "tm", axis=0, tiled=True), time_steps), tile_ids
    )
    return summed * inverse_count


def solution(mesh):
    in_specs = (P("freq", "tm", None, None), P())
    out_specs = P("tm", "freq", None, None, None)
    return jax.shard_map(
        on_device, mesh=mesh, in_specs=in_specs, out_specs=out_specs, check_vma=False
    )
```

```python
import math

import jax
import jax.numpy as jnp
from jax import lax
from jax.experimental import pallas as pl
from jax.experimental.pallas import tpu as pltpu
from jax.sharding import PartitionSpec as P

NCHAN = 4096
TAPS = 4
TB = 128
CH_DEV = 2
C_BLOCK = 512


def passed_along(value, axis, steps):
    count = lax.axis_size(axis)
    leading, last = (max(0, -steps), min(count, count - steps))
    return lax.ppermute(value, axis, [(source, source + steps) for source in range(leading, last)])


def prototype_rows():
    sample_idx = jnp.arange(TAPS * NCHAN, dtype=jnp.int32)
    position = (sample_idx.astype(jnp.float32) + 0.5) / NCHAN - TAPS / 2.0
    hann_taper = 0.5 - 0.5 * jnp.cos(
        (sample_idx.astype(jnp.float32) + 0.5) * (2.0 * math.pi / (TAPS * NCHAN))
    )
    return (jnp.sinc(position) * hann_taper / (128.0 * math.sqrt(NCHAN))).reshape(TAPS, NCHAN)


def phase_tables(first_channel, channels):
    channel = first_channel + jnp.arange(channels, dtype=jnp.int32)
    step = 2.0 * math.pi / NCHAN
    lane = jnp.arange(C_BLOCK, dtype=jnp.int32)
    start = ((lane[None, :] * channel[:, None]) % NCHAN).astype(jnp.float32) * step
    cos_0, sin_0 = jnp.cos(start), jnp.sin(start)
    even = jnp.stack([cos_0, -sin_0], axis=1).reshape(2 * channels, C_BLOCK)
    odd = jnp.stack([sin_0, cos_0], axis=1).reshape(2 * channels, C_BLOCK)
    block = jnp.arange(NCHAN // C_BLOCK, dtype=jnp.int32) * C_BLOCK
    shift = ((block[:, None] * channel[None, :]) % NCHAN).astype(jnp.float32) * step
    cos_t = jnp.repeat(jnp.cos(shift), 2, axis=1)
    sin_t = jnp.repeat(jnp.sin(shift), 2, axis=1)
    turn = jnp.concatenate([cos_t, sin_t], axis=1)
    return jnp.concatenate([even, odd], axis=0), jnp.broadcast_to(turn[:, :, None], turn.shape + (128,))


def channelize_kernel(
    channels, fold_shift, proto_ref, first_ref, turn_ref, x_hbm, out_ref, buf, sems, acc_ref
):
    step = pl.program_id(0)
    count = pl.num_programs(0)
    cb = buf.shape[-1]

    def fetch(block, slot):
        for part in range(2):
            pltpu.make_async_copy(
                x_hbm.at[:, :, part, pl.ds(block * cb, cb)], buf.at[slot, part], sems.at[slot, part]
            ).start()

    @pl.when(step == 0)
    def _():
        fetch(0, 0)

    @pl.when(step + 1 < count)
    def _():
        fetch(step + 1, (step + 1) % 2)

    slot = step % 2
    for part in range(2):
        pltpu.make_async_copy(
            x_hbm.at[:, :, part, pl.ds(0, cb)], buf.at[slot, part], sems.at[slot, part]
        ).wait()
    turn = jnp.concatenate([turn_ref[...]] * (cb // turn_ref.shape[-1]), axis=1)
    even, odd = first_ref[: 2 * channels], first_ref[2 * channels :]
    cos_t, sin_t = turn[: 2 * channels], turn[2 * channels :]
    upper = even * cos_t - odd * sin_t
    lower = odd * cos_t + even * sin_t
    weights = proto_ref[...]
    re_tables = []
    im_tables = []
    for tap in range(TAPS):
        w = weights[tap : tap + 1, :]
        re_tables.append((w * upper).astype(jnp.bfloat16))
        im_tables.append((w * lower).astype(jnp.bfloat16))
    re_table = jnp.concatenate(re_tables, axis=0)
    im_table = jnp.concatenate(im_tables, axis=0)
    rows = buf.shape[2] * buf.shape[3]
    x_re = buf[slot, 0].reshape(rows, cb).astype(jnp.bfloat16)
    x_im = buf[slot, 1].reshape(rows, cb).astype(jnp.bfloat16)
    dims = (((1,), (1,)), ((), ()))
    part = lax.dot_general(x_re, re_table, dims, preferred_element_type=jnp.float32) + lax.dot_general(
        x_im, im_table, dims, preferred_element_type=jnp.float32
    )

    @pl.when(step == 0)
    def _():
        acc_ref[...] = part

    @pl.when(jnp.logical_and(step > 0, step < count - 1))
    def _():
        acc_ref[...] += part

    @pl.when(step == count - 1)
    def _():
        products = acc_ref[...] + part
        if not fold_shift:
            out_ref[...] = products
            return
        time_steps = buf.shape[3]
        width = 2 * channels
        block = lax.broadcasted_iota(jnp.int32, (rows, width), 0) % time_steps
        total = None
        for tap in range(TAPS):
            term = products[:, tap * width : (tap + 1) * width]
            lead = TAPS - 1 - tap
            if lead:
                term = jnp.where(block >= lead, pltpu.roll(term, lead, 0), 0.0)
            total = term if total is None else total + term
        out_ref[...] = total.T.astype(out_ref.dtype)


def tap_products(voltages, proto, first, turn, channels, fold_shift):
    local_inputs, time_steps = voltages.shape[0], voltages.shape[1]
    rows = local_inputs * time_steps
    width = TAPS * 2 * channels
    blocks = NCHAN // C_BLOCK
    kernel = lambda *refs: channelize_kernel(channels, fold_shift, *refs)
    if fold_shift:
        out_shape = jax.ShapeDtypeStruct((2 * channels, rows), jnp.bfloat16)
    else:
        out_shape = jax.ShapeDtypeStruct((rows, width), jnp.float32)
    return pl.pallas_call(
        kernel,
        out_shape=out_shape,
        grid=(blocks,),
        in_specs=[
            pl.BlockSpec((TAPS, C_BLOCK), lambda j: (0, j)),
            pl.BlockSpec((4 * channels, C_BLOCK), lambda j: (0, 0)),
            pl.BlockSpec((None, 4 * channels, 128), lambda j: (j, 0, 0)),
            pl.BlockSpec(memory_space=pl.ANY),
        ],
        out_specs=pl.BlockSpec(out_shape.shape, lambda j: (0, 0)),
        scratch_shapes=[
            pltpu.VMEM((2, 2, local_inputs, time_steps, C_BLOCK), jnp.int32),
            pltpu.SemaphoreType.DMA((2, 2)),
            pltpu.VMEM((rows, width), jnp.float32),
        ],
        compiler_params=pltpu.CompilerParams(
            dimension_semantics=("arbitrary",), vmem_limit_bytes=48 * 1024 * 1024
        ),
        cost_estimate=pl.CostEstimate(
            flops=2 * rows * 2 * NCHAN * width,
            transcendentals=0,
            bytes_accessed=voltages.size * 4 + rows * width * 4 + first.size * 4 + turn.size * 4,
        ),
    )(proto, first, turn, voltages)


def tile_coords(tile_id, blocks):
    step_row = jnp.arange(1, blocks, dtype=jnp.int32)
    triangle = step_row * (step_row + 1) // 2
    row_block = jnp.sum((tile_id[..., None] >= triangle).astype(jnp.int32), axis=-1)
    col_block = tile_id - row_block * (row_block + 1) // 2
    return (row_block, col_block)


def arrange_rows(gathered, time_steps):
    piece_count = gathered.shape[0]
    freq_count = gathered.shape[1]
    local_chans = gathered.shape[2]
    inner_width = gathered.shape[4] // time_steps
    unfolded = gathered.reshape(piece_count, freq_count, local_chans, 2, inner_width, time_steps)
    unfolded = unfolded.transpose(2, 3, 0, 5, 1, 4)
    return unfolded.reshape(local_chans, 2, piece_count * time_steps, freq_count * inner_width)


def tile_products(spectra, tile_ids):
    blocks = spectra.shape[3] // TB
    row_block, col_block = tile_coords(tile_ids, blocks)
    shaped = spectra.reshape(spectra.shape[0], 2, spectra.shape[2], blocks, TB)
    row_tiles = jnp.take(shaped, row_block, axis=3)
    col_tiles = jnp.take(shaped, col_block, axis=3)
    turned = jnp.stack([row_tiles[:, 1], -row_tiles[:, 0]], axis=1)
    paired = jnp.stack([row_tiles, turned], axis=1)
    return jnp.einsum("hqptsx,hptsy->shqxy", paired, col_tiles, preferred_element_type=jnp.float32)


def on_device(voltages, tile_map):
    local_inputs = voltages.shape[0]
    time_steps = voltages.shape[1]
    freq_devices = lax.axis_size("freq")
    time_devices = lax.axis_size("tm")
    channels = CH_DEV * freq_devices
    first_channel = NCHAN // 2 - channels // 2
    proto = prototype_rows()
    first, turn = phase_tables(first_channel, channels)
    if time_devices == 1:
        spectra = tap_products(voltages, proto, first, turn, channels, True)
    else:
        products = tap_products(voltages, proto, first, turn, channels, False)
        products = products.reshape(local_inputs, time_steps, TAPS, 2 * channels)
        tail = products[:, time_steps - (TAPS - 1) :]
        previous = passed_along(tail, "tm", 1)
        total = None
        for tap in range(TAPS):
            lead = TAPS - 1 - tap
            shifted = jnp.concatenate(
                [previous[:, tap:, tap], products[:, : time_steps - lead, tap]], axis=1
            )
            total = shifted if total is None else total + shifted
        spectra = total.astype(jnp.bfloat16).reshape(local_inputs * time_steps, 2 * channels).T
    spectra = spectra.reshape(freq_devices, CH_DEV, 2, local_inputs * time_steps)
    turned = lax.all_to_all(spectra, "freq", split_axis=0, concat_axis=0, tiled=True)
    slot_count = tile_map.shape[0] // time_devices
    inverse_count = 1.0 / (time_steps * time_devices)
    tile_ids = lax.dynamic_slice_in_dim(tile_map, lax.axis_index("tm") * slot_count, slot_count)
    summed = tile_products(
        arrange_rows(lax.all_gather(turned[None], "tm", axis=0, tiled=True), time_steps), tile_ids
    )
    return summed * inverse_count


def solution(mesh):
    in_specs = (P("freq", "tm", None, None), P())
    out_specs = P("tm", "freq", None, None, None)
    return jax.shard_map(
        on_device, mesh=mesh, in_specs=in_specs, out_specs=out_specs, check_vma=False
    )
```

```python
import math

import jax
import jax.numpy as jnp
from jax import lax
from jax.experimental import pallas as pl
from jax.experimental.pallas import tpu as pltpu
from jax.sharding import PartitionSpec as P

NCHAN = 4096
TAPS = 4
TB = 128
CH_DEV = 2
C_BLOCK = 512


def passed_along(value, axis, steps):
    count = lax.axis_size(axis)
    leading, last = (max(0, -steps), min(count, count - steps))
    return lax.ppermute(value, axis, [(source, source + steps) for source in range(leading, last)])


def prototype_rows():
    sample_idx = jnp.arange(TAPS * NCHAN, dtype=jnp.int32)
    position = (sample_idx.astype(jnp.float32) + 0.5) / NCHAN - TAPS / 2.0
    hann_taper = 0.5 - 0.5 * jnp.cos(
        (sample_idx.astype(jnp.float32) + 0.5) * (2.0 * math.pi / (TAPS * NCHAN))
    )
    return (jnp.sinc(position) * hann_taper / (128.0 * math.sqrt(NCHAN))).reshape(TAPS, NCHAN)


def phase_tables(first_channel, channels):
    rows = 4 * channels
    step = 2.0 * math.pi / NCHAN
    quarter = NCHAN // 4
    row = lax.broadcasted_iota(jnp.int32, (rows, C_BLOCK), 0)
    lane = lax.broadcasted_iota(jnp.int32, (rows, C_BLOCK), 1)
    channel = first_channel + (row % (2 * channels)) // 2
    part = row % 2
    offset = jnp.where(row >= 2 * channels, (1 - part) * 3 * quarter, part * quarter)
    first = jnp.cos(((lane * channel + offset) % NCHAN).astype(jnp.float32) * step)
    blocks = NCHAN // C_BLOCK
    block = lax.broadcasted_iota(jnp.int32, (blocks, rows), 0) * C_BLOCK
    row = lax.broadcasted_iota(jnp.int32, (blocks, rows), 1)
    channel = first_channel + (row % (2 * channels)) // 2
    offset = jnp.where(row >= 2 * channels, 3 * quarter, 0)
    turn = jnp.cos(((block * channel + offset) % NCHAN).astype(jnp.float32) * step)
    return first, jnp.broadcast_to(turn[:, :, None], (blocks, rows, 128))


def channelize_kernel(
    channels, fold_shift, proto_ref, first_ref, turn_ref, x_hbm, out_ref, buf, sems, acc_ref
):
    step = pl.program_id(0)
    count = pl.num_programs(0)
    cb = buf.shape[-1]

    def fetch(block, slot):
        for part in range(2):
            pltpu.make_async_copy(
                x_hbm.at[:, :, part, pl.ds(block * cb, cb)], buf.at[slot, part], sems.at[slot, part]
            ).start()

    @pl.when(step == 0)
    def _():
        fetch(0, 0)

    @pl.when(step + 1 < count)
    def _():
        fetch(step + 1, (step + 1) % 2)

    slot = step % 2
    for part in range(2):
        pltpu.make_async_copy(
            x_hbm.at[:, :, part, pl.ds(0, cb)], buf.at[slot, part], sems.at[slot, part]
        ).wait()
    turn = jnp.concatenate([turn_ref[...]] * (cb // turn_ref.shape[-1]), axis=1)
    even, odd = first_ref[: 2 * channels], first_ref[2 * channels :]
    cos_t, sin_t = turn[: 2 * channels], turn[2 * channels :]
    upper = even * cos_t - odd * sin_t
    lower = odd * cos_t + even * sin_t
    weights = proto_ref[...]
    re_tables = []
    im_tables = []
    for tap in range(TAPS):
        w = weights[tap : tap + 1, :]
        re_tables.append((w * upper).astype(jnp.bfloat16))
        im_tables.append((w * lower).astype(jnp.bfloat16))
    re_table = jnp.concatenate(re_tables, axis=0)
    im_table = jnp.concatenate(im_tables, axis=0)
    rows = buf.shape[2] * buf.shape[3]
    x_re = buf[slot, 0].reshape(rows, cb).astype(jnp.bfloat16)
    x_im = buf[slot, 1].reshape(rows, cb).astype(jnp.bfloat16)
    dims = (((1,), (1,)), ((), ()))
    part = lax.dot_general(x_re, re_table, dims, preferred_element_type=jnp.float32) + lax.dot_general(
        x_im, im_table, dims, preferred_element_type=jnp.float32
    )

    @pl.when(step == 0)
    def _():
        acc_ref[...] = part

    @pl.when(jnp.logical_and(step > 0, step < count - 1))
    def _():
        acc_ref[...] += part

    @pl.when(step == count - 1)
    def _():
        products = acc_ref[...] + part
        if not fold_shift:
            out_ref[...] = products
            return
        time_steps = buf.shape[3]
        width = 2 * channels
        block = lax.broadcasted_iota(jnp.int32, (rows, width), 0) % time_steps
        total = None
        for tap in range(TAPS):
            term = products[:, tap * width : (tap + 1) * width]
            lead = TAPS - 1 - tap
            if lead:
                term = jnp.where(block >= lead, pltpu.roll(term, lead, 0), 0.0)
            total = term if total is None else total + term
        out_ref[...] = total.T.astype(out_ref.dtype)


def tap_products(voltages, proto, first, turn, channels, fold_shift):
    local_inputs, time_steps = voltages.shape[0], voltages.shape[1]
    rows = local_inputs * time_steps
    width = TAPS * 2 * channels
    blocks = NCHAN // C_BLOCK
    kernel = lambda *refs: channelize_kernel(channels, fold_shift, *refs)
    if fold_shift:
        out_shape = jax.ShapeDtypeStruct((2 * channels, rows), jnp.bfloat16)
    else:
        out_shape = jax.ShapeDtypeStruct((rows, width), jnp.float32)
    return pl.pallas_call(
        kernel,
        out_shape=out_shape,
        grid=(blocks,),
        in_specs=[
            pl.BlockSpec((TAPS, C_BLOCK), lambda j: (0, j)),
            pl.BlockSpec((4 * channels, C_BLOCK), lambda j: (0, 0)),
            pl.BlockSpec((None, 4 * channels, 128), lambda j: (j, 0, 0)),
            pl.BlockSpec(memory_space=pl.ANY),
        ],
        out_specs=pl.BlockSpec(out_shape.shape, lambda j: (0, 0)),
        scratch_shapes=[
            pltpu.VMEM((2, 2, local_inputs, time_steps, C_BLOCK), jnp.int32),
            pltpu.SemaphoreType.DMA((2, 2)),
            pltpu.VMEM((rows, width), jnp.float32),
        ],
        compiler_params=pltpu.CompilerParams(
            dimension_semantics=("arbitrary",), vmem_limit_bytes=48 * 1024 * 1024
        ),
        cost_estimate=pl.CostEstimate(
            flops=2 * rows * 2 * NCHAN * width,
            transcendentals=0,
            bytes_accessed=voltages.size * 4 + rows * width * 4 + first.size * 4 + turn.size * 4,
        ),
    )(proto, first, turn, voltages)


def tile_coords(tile_id, blocks):
    step_row = jnp.arange(1, blocks, dtype=jnp.int32)
    triangle = step_row * (step_row + 1) // 2
    row_block = jnp.sum((tile_id[..., None] >= triangle).astype(jnp.int32), axis=-1)
    col_block = tile_id - row_block * (row_block + 1) // 2
    return (row_block, col_block)


def arrange_rows(gathered, time_steps):
    piece_count = gathered.shape[0]
    freq_count = gathered.shape[1]
    local_chans = gathered.shape[2]
    inner_width = gathered.shape[4] // time_steps
    unfolded = gathered.reshape(piece_count, freq_count, local_chans, 2, inner_width, time_steps)
    unfolded = unfolded.transpose(2, 3, 0, 5, 1, 4)
    return unfolded.reshape(local_chans, 2, piece_count * time_steps, freq_count * inner_width)


def tile_products(spectra, tile_ids):
    blocks = spectra.shape[3] // TB
    row_block, col_block = tile_coords(tile_ids, blocks)
    shaped = spectra.reshape(spectra.shape[0], 2, spectra.shape[2], blocks, TB)
    row_tiles = jnp.take(shaped, row_block, axis=3)
    col_tiles = jnp.take(shaped, col_block, axis=3)
    turned = jnp.stack([row_tiles[:, 1], -row_tiles[:, 0]], axis=1)
    paired = jnp.stack([row_tiles, turned], axis=1)
    return jnp.einsum("hqptsx,hptsy->shqxy", paired, col_tiles, preferred_element_type=jnp.float32)


def on_device(voltages, tile_map):
    local_inputs = voltages.shape[0]
    time_steps = voltages.shape[1]
    freq_devices = lax.axis_size("freq")
    time_devices = lax.axis_size("tm")
    channels = CH_DEV * freq_devices
    first_channel = NCHAN // 2 - channels // 2
    proto = prototype_rows()
    first, turn = phase_tables(first_channel, channels)
    if time_devices == 1:
        spectra = tap_products(voltages, proto, first, turn, channels, True)
    else:
        products = tap_products(voltages, proto, first, turn, channels, False)
        products = products.reshape(local_inputs, time_steps, TAPS, 2 * channels)
        tail = products[:, time_steps - (TAPS - 1) :]
        previous = passed_along(tail, "tm", 1)
        total = None
        for tap in range(TAPS):
            lead = TAPS - 1 - tap
            shifted = jnp.concatenate(
                [previous[:, tap:, tap], products[:, : time_steps - lead, tap]], axis=1
            )
            total = shifted if total is None else total + shifted
        spectra = total.astype(jnp.bfloat16).reshape(local_inputs * time_steps, 2 * channels).T
    spectra = spectra.reshape(freq_devices, CH_DEV, 2, local_inputs * time_steps)
    turned = lax.all_to_all(spectra, "freq", split_axis=0, concat_axis=0, tiled=True)
    slot_count = tile_map.shape[0] // time_devices
    inverse_count = 1.0 / (time_steps * time_devices)
    tile_ids = lax.dynamic_slice_in_dim(tile_map, lax.axis_index("tm") * slot_count, slot_count)
    summed = tile_products(
        arrange_rows(lax.all_gather(turned[None], "tm", axis=0, tiled=True), time_steps), tile_ids
    )
    return summed * inverse_count


def solution(mesh):
    in_specs = (P("freq", "tm", None, None), P())
    out_specs = P("tm", "freq", None, None, None)
    return jax.shard_map(
        on_device, mesh=mesh, in_specs=in_specs, out_specs=out_specs, check_vma=False
    )
```

```python
import math

import jax
import jax.numpy as jnp
from jax import lax
from jax.experimental import pallas as pl
from jax.experimental.pallas import tpu as pltpu
from jax.sharding import PartitionSpec as P

NCHAN = 4096
TAPS = 4
TB = 128
CH_DEV = 2
C_BLOCK = 512


def passed_along(value, axis, steps):
    count = lax.axis_size(axis)
    leading, last = (max(0, -steps), min(count, count - steps))
    return lax.ppermute(value, axis, [(source, source + steps) for source in range(leading, last)])


def prototype_rows():
    sample_idx = jnp.arange(TAPS * NCHAN, dtype=jnp.int32)
    position = (sample_idx.astype(jnp.float32) + 0.5) / NCHAN - TAPS / 2.0
    hann_taper = 0.5 - 0.5 * jnp.cos(
        (sample_idx.astype(jnp.float32) + 0.5) * (2.0 * math.pi / (TAPS * NCHAN))
    )
    return (jnp.sinc(position) * hann_taper / (128.0 * math.sqrt(NCHAN))).reshape(TAPS, NCHAN)


def phase_tables(first_channel, channels):
    channel = first_channel + jnp.arange(channels, dtype=jnp.int32)
    step = 2.0 * math.pi / NCHAN
    lane = jnp.arange(C_BLOCK, dtype=jnp.int32)
    start = ((lane[None, :] * channel[:, None]) % NCHAN).astype(jnp.float32) * step
    cos_0, sin_0 = jnp.cos(start), jnp.sin(start)
    even = jnp.stack([cos_0, -sin_0], axis=1).reshape(2 * channels, C_BLOCK)
    odd = jnp.stack([sin_0, cos_0], axis=1).reshape(2 * channels, C_BLOCK)
    block = jnp.arange(NCHAN // C_BLOCK, dtype=jnp.int32) * C_BLOCK
    shift = ((block[:, None] * channel[None, :]) % NCHAN).astype(jnp.float32) * step
    cos_t = jnp.repeat(jnp.cos(shift), 2, axis=1)
    sin_t = jnp.repeat(jnp.sin(shift), 2, axis=1)
    turn = jnp.concatenate([cos_t, sin_t], axis=1)
    return jnp.concatenate([even, odd], axis=0), jnp.broadcast_to(turn[:, :, None], turn.shape + (128,))


def channelize_kernel(
    channels, fold_shift, proto_ref, first_ref, turn_ref, x_hbm, out_ref, buf, sems, acc_ref
):
    step = pl.program_id(0)
    count = pl.num_programs(0)
    cb = buf.shape[-1]

    def fetch(block, slot):
        for part in range(2):
            pltpu.make_async_copy(
                x_hbm.at[:, :, part, pl.ds(block * cb, cb)], buf.at[slot, part], sems.at[slot, part]
            ).start()

    @pl.when(step == 0)
    def _():
        fetch(0, 0)

    @pl.when(step + 1 < count)
    def _():
        fetch(step + 1, (step + 1) % 2)

    slot = step % 2
    for part in range(2):
        pltpu.make_async_copy(
            x_hbm.at[:, :, part, pl.ds(0, cb)], buf.at[slot, part], sems.at[slot, part]
        ).wait()
    turn = jnp.concatenate([turn_ref[...]] * (cb // turn_ref.shape[-1]), axis=1)
    even, odd = first_ref[: 2 * channels], first_ref[2 * channels :]
    cos_t, sin_t = turn[: 2 * channels], turn[2 * channels :]
    upper = even * cos_t - odd * sin_t
    lower = odd * cos_t + even * sin_t
    weights = proto_ref[...]
    re_tables = []
    im_tables = []
    for tap in range(TAPS):
        w = weights[tap : tap + 1, :]
        re_tables.append((w * upper).astype(jnp.bfloat16))
        im_tables.append((w * lower).astype(jnp.bfloat16))
    re_table = jnp.concatenate(re_tables, axis=0)
    im_table = jnp.concatenate(im_tables, axis=0)
    rows = buf.shape[2] * buf.shape[3]
    x_re = buf[slot, 0].reshape(rows, cb).astype(jnp.bfloat16)
    x_im = buf[slot, 1].reshape(rows, cb).astype(jnp.bfloat16)
    dims = (((1,), (1,)), ((), ()))
    part = lax.dot_general(x_re, re_table, dims, preferred_element_type=jnp.float32) + lax.dot_general(
        x_im, im_table, dims, preferred_element_type=jnp.float32
    )

    @pl.when(step == 0)
    def _():
        acc_ref[...] = part

    @pl.when(jnp.logical_and(step > 0, step < count - 1))
    def _():
        acc_ref[...] += part

    @pl.when(step == count - 1)
    def _():
        products = acc_ref[...] + part
        if not fold_shift:
            out_ref[...] = products
            return
        time_steps = buf.shape[3]
        width = 2 * channels
        block = lax.broadcasted_iota(jnp.int32, (rows, width), 0) % time_steps
        total = None
        for tap in range(TAPS):
            term = products[:, tap * width : (tap + 1) * width]
            lead = TAPS - 1 - tap
            if lead:
                term = jnp.where(block >= lead, pltpu.roll(term, lead, 0), 0.0)
            total = term if total is None else total + term
        out_ref[...] = total.T.astype(out_ref.dtype)


def tap_products(voltages, proto, first, turn, channels, fold_shift):
    local_inputs, time_steps = voltages.shape[0], voltages.shape[1]
    rows = local_inputs * time_steps
    width = TAPS * 2 * channels
    blocks = NCHAN // C_BLOCK
    kernel = lambda *refs: channelize_kernel(channels, fold_shift, *refs)
    if fold_shift:
        out_shape = jax.ShapeDtypeStruct((2 * channels, rows), jnp.bfloat16)
    else:
        out_shape = jax.ShapeDtypeStruct((rows, width), jnp.float32)
    return pl.pallas_call(
        kernel,
        out_shape=out_shape,
        grid=(blocks,),
        in_specs=[
            pl.BlockSpec((TAPS, C_BLOCK), lambda j: (0, j)),
            pl.BlockSpec((4 * channels, C_BLOCK), lambda j: (0, 0)),
            pl.BlockSpec((None, 4 * channels, 128), lambda j: (j, 0, 0)),
            pl.BlockSpec(memory_space=pl.ANY),
        ],
        out_specs=pl.BlockSpec(out_shape.shape, lambda j: (0, 0)),
        scratch_shapes=[
            pltpu.VMEM((2, 2, local_inputs, time_steps, C_BLOCK), jnp.int32),
            pltpu.SemaphoreType.DMA((2, 2)),
            pltpu.VMEM((rows, width), jnp.float32),
        ],
        compiler_params=pltpu.CompilerParams(
            dimension_semantics=("arbitrary",), vmem_limit_bytes=48 * 1024 * 1024
        ),
        cost_estimate=pl.CostEstimate(
            flops=2 * rows * 2 * NCHAN * width,
            transcendentals=0,
            bytes_accessed=voltages.size * 4 + rows * width * 4 + first.size * 4 + turn.size * 4,
        ),
    )(proto, first, turn, voltages)


def tile_coords(tile_id, blocks):
    step_row = jnp.arange(1, blocks, dtype=jnp.int32)
    triangle = step_row * (step_row + 1) // 2
    row_block = jnp.sum((tile_id[..., None] >= triangle).astype(jnp.int32), axis=-1)
    col_block = tile_id - row_block * (row_block + 1) // 2
    return (row_block, col_block)


def arrange_rows(gathered, time_steps):
    piece_count = gathered.shape[0]
    freq_count = gathered.shape[1]
    local_chans = gathered.shape[2]
    inner_width = gathered.shape[4] // time_steps
    unfolded = gathered.reshape(piece_count, freq_count, local_chans, 2, inner_width, time_steps)
    unfolded = unfolded.transpose(2, 3, 0, 5, 1, 4)
    return unfolded.reshape(local_chans, 2, piece_count * time_steps, freq_count * inner_width)


def correlate_kernel(blocks, tiles_per_step, scale, ids_ref, lhs_ref, rhs_ref, out_ref):
    step = pl.program_id(0)
    for slot in range(tiles_per_step):
        tile_id = ids_ref[step * tiles_per_step + slot]
        row_block = jnp.int32(0)
        for r in range(1, blocks):
            row_block = row_block + (tile_id >= r * (r + 1) // 2).astype(jnp.int32)
        col_block = tile_id - row_block * (row_block + 1) // 2
        rows = pl.ds(pl.multiple_of(row_block * TB, TB), TB)
        cols = pl.ds(pl.multiple_of(col_block * TB, TB), TB)
        for chan in range(lhs_ref.shape[0]):
            right = rhs_ref[chan, :, cols]
            for part in range(2):
                left = lhs_ref[chan, part, rows, :]
                product = jnp.dot(left, right, preferred_element_type=jnp.float32)
                out_ref[slot, chan, part] = product * scale


def tile_products(spectra, tile_ids, scale):
    local_chans, depth, paths = spectra.shape
    blocks = paths // TB
    half = depth // 2
    turned_rows = spectra.transpose(0, 2, 1)
    rotated = jnp.concatenate([turned_rows[:, :, half:], -turned_rows[:, :, :half]], axis=2)
    lhs = jnp.stack([turned_rows, rotated], axis=1)
    count = tile_ids.shape[0]
    tiles_per_step = max(d for d in range(1, 10) if count % d == 0)
    kernel = lambda *refs: correlate_kernel(blocks, tiles_per_step, scale, *refs)
    out_block = (tiles_per_step, local_chans, 2, TB, TB)
    return pl.pallas_call(
        kernel,
        out_shape=jax.ShapeDtypeStruct((count, local_chans, 2, TB, TB), jnp.float32),
        grid_spec=pltpu.PrefetchScalarGridSpec(
            num_scalar_prefetch=1,
            grid=(count // tiles_per_step,),
            in_specs=[
                pl.BlockSpec(lhs.shape, lambda j, ids: (0, 0, 0, 0)),
                pl.BlockSpec(spectra.shape, lambda j, ids: (0, 0, 0)),
            ],
            out_specs=pl.BlockSpec(out_block, lambda j, ids: (j, 0, 0, 0, 0)),
        ),
        compiler_params=pltpu.CompilerParams(
            dimension_semantics=("arbitrary",), vmem_limit_bytes=48 * 1024 * 1024
        ),
        cost_estimate=pl.CostEstimate(
            flops=2 * count * local_chans * 2 * TB * TB * depth,
            transcendentals=0,
            bytes_accessed=count * local_chans * 2 * TB * TB * 4 + lhs.size * 2 + spectra.size * 2,
        ),
    )(tile_ids, lhs, spectra)


def on_device(voltages, tile_map):
    local_inputs = voltages.shape[0]
    time_steps = voltages.shape[1]
    freq_devices = lax.axis_size("freq")
    time_devices = lax.axis_size("tm")
    channels = CH_DEV * freq_devices
    first_channel = NCHAN // 2 - channels // 2
    proto = prototype_rows()
    first, turn = phase_tables(first_channel, channels)
    if time_devices == 1:
        spectra = tap_products(voltages, proto, first, turn, channels, True)
    else:
        products = tap_products(voltages, proto, first, turn, channels, False)
        products = products.reshape(local_inputs, time_steps, TAPS, 2 * channels)
        tail = products[:, time_steps - (TAPS - 1) :]
        previous = passed_along(tail, "tm", 1)
        total = None
        for tap in range(TAPS):
            lead = TAPS - 1 - tap
            shifted = jnp.concatenate(
                [previous[:, tap:, tap], products[:, : time_steps - lead, tap]], axis=1
            )
            total = shifted if total is None else total + shifted
        spectra = total.astype(jnp.bfloat16).reshape(local_inputs * time_steps, 2 * channels).T
    spectra = spectra.reshape(freq_devices, CH_DEV, 2, local_inputs * time_steps)
    turned = lax.all_to_all(spectra, "freq", split_axis=0, concat_axis=0, tiled=True)
    slot_count = tile_map.shape[0] // time_devices
    inverse_count = 1.0 / (time_steps * time_devices)
    tile_ids = lax.dynamic_slice_in_dim(tile_map, lax.axis_index("tm") * slot_count, slot_count)
    arranged = arrange_rows(lax.all_gather(turned[None], "tm", axis=0, tiled=True), time_steps)
    arranged = arranged.reshape(arranged.shape[0], -1, arranged.shape[3])
    return tile_products(arranged, tile_ids, inverse_count)


def solution(mesh):
    in_specs = (P("freq", "tm", None, None), P())
    out_specs = P("tm", "freq", None, None, None)
    return jax.shard_map(
        on_device, mesh=mesh, in_specs=in_specs, out_specs=out_specs, check_vma=False
    )
```

```python
import math

import jax
import jax.numpy as jnp
from jax import lax
from jax.experimental import pallas as pl
from jax.experimental.pallas import tpu as pltpu
from jax.sharding import PartitionSpec as P

NCHAN = 4096
TAPS = 4
TB = 128
CH_DEV = 2
C_BLOCK = 512


def passed_along(value, axis, steps):
    count = lax.axis_size(axis)
    leading, last = (max(0, -steps), min(count, count - steps))
    return lax.ppermute(value, axis, [(source, source + steps) for source in range(leading, last)])


def prototype_rows():
    sample_idx = jnp.arange(TAPS * NCHAN, dtype=jnp.int32)
    position = (sample_idx.astype(jnp.float32) + 0.5) / NCHAN - TAPS / 2.0
    hann_taper = 0.5 - 0.5 * jnp.cos(
        (sample_idx.astype(jnp.float32) + 0.5) * (2.0 * math.pi / (TAPS * NCHAN))
    )
    return (jnp.sinc(position) * hann_taper / (128.0 * math.sqrt(NCHAN))).reshape(TAPS, NCHAN)


def phase_tables(first_channel, channels):
    channel = first_channel + jnp.arange(channels, dtype=jnp.int32)
    step = 2.0 * math.pi / NCHAN
    lane = jnp.arange(C_BLOCK, dtype=jnp.int32)
    start = ((lane[None, :] * channel[:, None]) % NCHAN).astype(jnp.float32) * step
    first = jnp.concatenate([jnp.cos(start), jnp.sin(start)], axis=0)
    block = jnp.arange(NCHAN // C_BLOCK, dtype=jnp.int32) * C_BLOCK
    shift = ((block[:, None] * channel[None, :]) % NCHAN).astype(jnp.float32) * step
    turn = jnp.concatenate([jnp.cos(shift), jnp.sin(shift)], axis=1)
    return first, jnp.broadcast_to(turn[:, :, None], turn.shape + (128,))


def channelize_kernel(
    channels, fold_shift, proto_ref, first_ref, turn_ref, x_hbm, out_ref, buf, sems, acc_ref, *scratch
):
    step = pl.program_id(0)
    count = pl.num_programs(0)
    cb = buf.shape[-1]

    def fetch(block, slot):
        for part in range(2):
            pltpu.make_async_copy(
                x_hbm.at[:, :, part, pl.ds(block * cb, cb)], buf.at[slot, part], sems.at[slot, part]
            ).start()

    @pl.when(step == 0)
    def _():
        fetch(0, 0)

    @pl.when(step + 1 < count)
    def _():
        fetch(step + 1, (step + 1) % 2)

    slot = step % 2
    for part in range(2):
        pltpu.make_async_copy(
            x_hbm.at[:, :, part, pl.ds(0, cb)], buf.at[slot, part], sems.at[slot, part]
        ).wait()
    turn = jnp.concatenate([turn_ref[...]] * (cb // turn_ref.shape[-1]), axis=1)
    cos_0, sin_0 = first_ref[:channels], first_ref[channels:]
    cos_t, sin_t = turn[:channels], turn[channels:]
    cosine = cos_0 * cos_t - sin_0 * sin_t
    sine = sin_0 * cos_t + cos_0 * sin_t
    upper = jnp.concatenate([cosine, -sine], axis=0)
    lower = jnp.concatenate([sine, cosine], axis=0)
    weights = proto_ref[...]
    re_tables = []
    im_tables = []
    for tap in range(TAPS):
        w = weights[tap : tap + 1, :]
        re_tables.append((w * upper).astype(jnp.bfloat16))
        im_tables.append((w * lower).astype(jnp.bfloat16))
    re_table = jnp.concatenate(re_tables, axis=0)
    im_table = jnp.concatenate(im_tables, axis=0)
    rows = buf.shape[2] * buf.shape[3]
    x_re = buf[slot, 0].reshape(rows, cb).astype(jnp.bfloat16)
    x_im = buf[slot, 1].reshape(rows, cb).astype(jnp.bfloat16)
    dims = (((1,), (1,)), ((), ()))
    part = lax.dot_general(x_re, re_table, dims, preferred_element_type=jnp.float32) + lax.dot_general(
        x_im, im_table, dims, preferred_element_type=jnp.float32
    )

    @pl.when(step == 0)
    def _():
        acc_ref[...] = part

    @pl.when(jnp.logical_and(step > 0, step < count - 1))
    def _():
        acc_ref[...] += part

    @pl.when(step == count - 1)
    def _():
        products = acc_ref[...] + part
        if not fold_shift:
            out_ref[...] = products
            return
        time_steps = buf.shape[3]
        width = 2 * channels
        block = lax.broadcasted_iota(jnp.int32, (rows, width), 0) % time_steps
        total = None
        for tap in range(TAPS):
            term = products[:, tap * width : (tap + 1) * width]
            lead = TAPS - 1 - tap
            if lead:
                term = jnp.where(block >= lead, pltpu.roll(term, lead, 0), 0.0)
            total = term if total is None else total + term
        (staged,) = scratch
        lanes = staged.shape[-1]
        for half in range(2):
            rows_q = pl.ds(half, channels, stride=2)
            flipped = total[:, half * channels : (half + 1) * channels].T
            for chunk in range(staged.shape[0]):
                staged[chunk, rows_q, :] = flipped[:, chunk * lanes : (chunk + 1) * lanes]
        for chunk in range(staged.shape[0]):
            out_ref[:, chunk * lanes : (chunk + 1) * lanes] = staged[chunk].astype(out_ref.dtype)


def tap_products(voltages, proto, first, turn, channels, fold_shift):
    local_inputs, time_steps = voltages.shape[0], voltages.shape[1]
    rows = local_inputs * time_steps
    width = TAPS * 2 * channels
    blocks = NCHAN // C_BLOCK
    kernel = lambda *refs: channelize_kernel(channels, fold_shift, *refs)
    if fold_shift:
        out_shape = jax.ShapeDtypeStruct((2 * channels, rows), jnp.bfloat16)
    else:
        out_shape = jax.ShapeDtypeStruct((rows, width), jnp.float32)
    return pl.pallas_call(
        kernel,
        out_shape=out_shape,
        grid=(blocks,),
        in_specs=[
            pl.BlockSpec((TAPS, C_BLOCK), lambda j: (0, j)),
            pl.BlockSpec((2 * channels, C_BLOCK), lambda j: (0, 0)),
            pl.BlockSpec((None, 2 * channels, 128), lambda j: (j, 0, 0)),
            pl.BlockSpec(memory_space=pl.ANY),
        ],
        out_specs=pl.BlockSpec(out_shape.shape, lambda j: (0, 0)),
        scratch_shapes=[
            pltpu.VMEM((2, 2, local_inputs, time_steps, C_BLOCK), jnp.int32),
            pltpu.SemaphoreType.DMA((2, 2)),
            pltpu.VMEM((rows, width), jnp.float32),
        ]
        + ([pltpu.VMEM((rows // 128, 2 * channels, 128), jnp.float32)] if fold_shift else []),
        compiler_params=pltpu.CompilerParams(
            dimension_semantics=("arbitrary",), vmem_limit_bytes=48 * 1024 * 1024
        ),
        cost_estimate=pl.CostEstimate(
            flops=2 * rows * 2 * NCHAN * width,
            transcendentals=0,
            bytes_accessed=voltages.size * 4 + rows * width * 4 + first.size * 4 + turn.size * 4,
        ),
    )(proto, first, turn, voltages)


def tile_coords(tile_id, blocks):
    step_row = jnp.arange(1, blocks, dtype=jnp.int32)
    triangle = step_row * (step_row + 1) // 2
    row_block = jnp.sum((tile_id[..., None] >= triangle).astype(jnp.int32), axis=-1)
    col_block = tile_id - row_block * (row_block + 1) // 2
    return (row_block, col_block)


def arrange_rows(gathered, time_steps):
    piece_count = gathered.shape[0]
    freq_count = gathered.shape[1]
    local_chans = gathered.shape[2]
    inner_width = gathered.shape[4] // time_steps
    unfolded = gathered.reshape(piece_count, freq_count, local_chans, 2, inner_width, time_steps)
    unfolded = unfolded.transpose(2, 3, 0, 5, 1, 4)
    return unfolded.reshape(local_chans, 2, piece_count * time_steps, freq_count * inner_width)


def correlate_kernel(blocks, tiles_per_step, scale, ids_ref, lhs_ref, rhs_ref, out_ref):
    step = pl.program_id(0)
    for slot in range(tiles_per_step):
        tile_id = ids_ref[step * tiles_per_step + slot]
        row_block = jnp.int32(0)
        for r in range(1, blocks):
            row_block = row_block + (tile_id >= r * (r + 1) // 2).astype(jnp.int32)
        col_block = tile_id - row_block * (row_block + 1) // 2
        rows = pl.ds(pl.multiple_of(row_block * TB, TB), TB)
        cols = pl.ds(pl.multiple_of(col_block * TB, TB), TB)
        for chan in range(lhs_ref.shape[0]):
            right = rhs_ref[chan, :, cols]
            for part in range(2):
                left = lhs_ref[chan, part, rows, :]
                product = jnp.dot(left, right, preferred_element_type=jnp.float32)
                out_ref[slot, chan, part] = product


def tile_products(spectra, tile_ids, scale):
    local_chans, depth, paths = spectra.shape
    blocks = paths // TB
    half = depth // 2
    turned_rows = spectra.transpose(0, 2, 1)
    rotated = jnp.concatenate([turned_rows[:, :, half:], -turned_rows[:, :, :half]], axis=2)
    lhs = (jnp.stack([turned_rows, rotated], axis=1) * scale).astype(spectra.dtype)
    count = tile_ids.shape[0]
    tiles_per_step = max(d for d in range(1, 7) if count % d == 0)
    kernel = lambda *refs: correlate_kernel(blocks, tiles_per_step, scale, *refs)
    out_block = (tiles_per_step, local_chans, 2, TB, TB)
    return pl.pallas_call(
        kernel,
        out_shape=jax.ShapeDtypeStruct((count, local_chans, 2, TB, TB), jnp.float32),
        grid_spec=pltpu.PrefetchScalarGridSpec(
            num_scalar_prefetch=1,
            grid=(count // tiles_per_step,),
            in_specs=[
                pl.BlockSpec(lhs.shape, lambda j, ids: (0, 0, 0, 0)),
                pl.BlockSpec(spectra.shape, lambda j, ids: (0, 0, 0)),
            ],
            out_specs=pl.BlockSpec(out_block, lambda j, ids: (j, 0, 0, 0, 0)),
        ),
        compiler_params=pltpu.CompilerParams(
            dimension_semantics=("arbitrary",), vmem_limit_bytes=48 * 1024 * 1024
        ),
        cost_estimate=pl.CostEstimate(
            flops=2 * count * local_chans * 2 * TB * TB * depth,
            transcendentals=0,
            bytes_accessed=count * local_chans * 2 * TB * TB * 4 + lhs.size * 2 + spectra.size * 2,
        ),
    )(tile_ids, lhs, spectra)


def on_device(voltages, tile_map):
    local_inputs = voltages.shape[0]
    time_steps = voltages.shape[1]
    freq_devices = lax.axis_size("freq")
    time_devices = lax.axis_size("tm")
    channels = CH_DEV * freq_devices
    first_channel = NCHAN // 2 - channels // 2
    proto = prototype_rows()
    first, turn = phase_tables(first_channel, channels)
    if time_devices == 1:
        spectra = tap_products(voltages, proto, first, turn, channels, True)
    else:
        products = tap_products(voltages, proto, first, turn, channels, False)
        products = products.reshape(local_inputs, time_steps, TAPS, 2 * channels)
        tail = products[:, time_steps - (TAPS - 1) :]
        previous = passed_along(tail, "tm", 1)
        total = None
        for tap in range(TAPS):
            lead = TAPS - 1 - tap
            shifted = jnp.concatenate(
                [previous[:, tap:, tap], products[:, : time_steps - lead, tap]], axis=1
            )
            total = shifted if total is None else total + shifted
        spectra = total.reshape(local_inputs * time_steps, 2, channels).transpose(2, 1, 0)
        spectra = spectra.astype(jnp.bfloat16)
    spectra = spectra.reshape(freq_devices, CH_DEV, 2, local_inputs * time_steps)
    turned = lax.all_to_all(spectra, "freq", split_axis=0, concat_axis=0, tiled=True)
    slot_count = tile_map.shape[0] // time_devices
    inverse_count = 1.0 / (time_steps * time_devices)
    tile_ids = lax.dynamic_slice_in_dim(tile_map, lax.axis_index("tm") * slot_count, slot_count)
    arranged = arrange_rows(lax.all_gather(turned[None], "tm", axis=0, tiled=True), time_steps)
    arranged = arranged.reshape(arranged.shape[0], -1, arranged.shape[3])
    return tile_products(arranged, tile_ids, inverse_count)


def solution(mesh):
    in_specs = (P("freq", "tm", None, None), P())
    out_specs = P("tm", "freq", None, None, None)
    return jax.shard_map(
        on_device, mesh=mesh, in_specs=in_specs, out_specs=out_specs, check_vma=False
    )
```

```python
import math

import jax
import jax.numpy as jnp
from jax import lax
from jax.experimental import pallas as pl
from jax.experimental.pallas import tpu as pltpu
from jax.sharding import PartitionSpec as P

NCHAN = 4096
TAPS = 4
TB = 128
CH_DEV = 2
C_BLOCK = 1024


def passed_along(value, axis, steps):
    count = lax.axis_size(axis)
    leading, last = (max(0, -steps), min(count, count - steps))
    return lax.ppermute(value, axis, [(source, source + steps) for source in range(leading, last)])


def prototype_rows():
    sample_idx = jnp.arange(TAPS * NCHAN, dtype=jnp.int32)
    position = (sample_idx.astype(jnp.float32) + 0.5) / NCHAN - TAPS / 2.0
    hann_taper = 0.5 - 0.5 * jnp.cos(
        (sample_idx.astype(jnp.float32) + 0.5) * (2.0 * math.pi / (TAPS * NCHAN))
    )
    return (jnp.sinc(position) * hann_taper / (128.0 * math.sqrt(NCHAN))).reshape(TAPS, NCHAN)


def phase_tables(first_channel, channels):
    channel = first_channel + jnp.arange(channels, dtype=jnp.int32)
    step = 2.0 * math.pi / NCHAN
    lane = jnp.arange(C_BLOCK, dtype=jnp.int32)
    start = ((lane[None, :] * channel[:, None]) % NCHAN).astype(jnp.float32) * step
    first = jnp.concatenate([jnp.cos(start), jnp.sin(start)], axis=0)
    block = jnp.arange(NCHAN // C_BLOCK, dtype=jnp.int32) * C_BLOCK
    shift = ((block[:, None] * channel[None, :]) % NCHAN).astype(jnp.float32) * step
    turn = jnp.concatenate([jnp.cos(shift), jnp.sin(shift)], axis=1)
    return first, jnp.broadcast_to(turn[:, :, None], turn.shape + (128,))


def channelize_kernel(
    channels, fold_shift, proto_ref, first_ref, turn_ref, x_hbm, out_ref, buf, sems, acc_ref, *scratch
):
    step = pl.program_id(0)
    count = pl.num_programs(0)
    cb = buf.shape[-1]

    def fetch(block, slot):
        for part in range(2):
            pltpu.make_async_copy(
                x_hbm.at[:, :, part, pl.ds(block * cb, cb)], buf.at[slot, part], sems.at[slot, part]
            ).start()

    @pl.when(step == 0)
    def _():
        fetch(0, 0)

    @pl.when(step + 1 < count)
    def _():
        fetch(step + 1, (step + 1) % 2)

    slot = step % 2
    for part in range(2):
        pltpu.make_async_copy(
            x_hbm.at[:, :, part, pl.ds(0, cb)], buf.at[slot, part], sems.at[slot, part]
        ).wait()
    turn = jnp.concatenate([turn_ref[...]] * (cb // turn_ref.shape[-1]), axis=1)
    cos_0, sin_0 = first_ref[:channels], first_ref[channels:]
    cos_t, sin_t = turn[:channels], turn[channels:]
    cosine = cos_0 * cos_t - sin_0 * sin_t
    sine = sin_0 * cos_t + cos_0 * sin_t
    upper = jnp.concatenate([cosine, -sine], axis=0)
    lower = jnp.concatenate([sine, cosine], axis=0)
    weights = proto_ref[...]
    re_tables = []
    im_tables = []
    for tap in range(TAPS):
        w = weights[tap : tap + 1, :]
        re_tables.append((w * upper).astype(jnp.bfloat16))
        im_tables.append((w * lower).astype(jnp.bfloat16))
    re_table = jnp.concatenate(re_tables, axis=0)
    im_table = jnp.concatenate(im_tables, axis=0)
    rows = buf.shape[2] * buf.shape[3]
    x_re = buf[slot, 0].reshape(rows, cb).astype(jnp.bfloat16)
    x_im = buf[slot, 1].reshape(rows, cb).astype(jnp.bfloat16)
    dims = (((1,), (1,)), ((), ()))
    part = lax.dot_general(x_re, re_table, dims, preferred_element_type=jnp.float32) + lax.dot_general(
        x_im, im_table, dims, preferred_element_type=jnp.float32
    )

    @pl.when(step == 0)
    def _():
        acc_ref[...] = part

    @pl.when(jnp.logical_and(step > 0, step < count - 1))
    def _():
        acc_ref[...] += part

    @pl.when(step == count - 1)
    def _():
        products = acc_ref[...] + part
        if not fold_shift:
            out_ref[...] = products
            return
        time_steps = buf.shape[3]
        width = 2 * channels
        block = lax.broadcasted_iota(jnp.int32, (rows, width), 0) % time_steps
        total = None
        for tap in range(TAPS):
            term = products[:, tap * width : (tap + 1) * width]
            lead = TAPS - 1 - tap
            if lead:
                term = jnp.where(block >= lead, pltpu.roll(term, lead, 0), 0.0)
            total = term if total is None else total + term
        (staged,) = scratch
        lanes = staged.shape[-1]
        for half in range(2):
            rows_q = pl.ds(half, channels, stride=2)
            flipped = total[:, half * channels : (half + 1) * channels].T
            for chunk in range(staged.shape[0]):
                staged[chunk, rows_q, :] = flipped[:, chunk * lanes : (chunk + 1) * lanes]
        for chunk in range(staged.shape[0]):
            out_ref[:, chunk * lanes : (chunk + 1) * lanes] = staged[chunk].astype(out_ref.dtype)


def tap_products(voltages, proto, first, turn, channels, fold_shift):
    local_inputs, time_steps = voltages.shape[0], voltages.shape[1]
    rows = local_inputs * time_steps
    width = TAPS * 2 * channels
    blocks = NCHAN // C_BLOCK
    kernel = lambda *refs: channelize_kernel(channels, fold_shift, *refs)
    if fold_shift:
        out_shape = jax.ShapeDtypeStruct((2 * channels, rows), jnp.bfloat16)
    else:
        out_shape = jax.ShapeDtypeStruct((rows, width), jnp.float32)
    return pl.pallas_call(
        kernel,
        out_shape=out_shape,
        grid=(blocks,),
        in_specs=[
            pl.BlockSpec((TAPS, C_BLOCK), lambda j: (0, j)),
            pl.BlockSpec((2 * channels, C_BLOCK), lambda j: (0, 0)),
            pl.BlockSpec((None, 2 * channels, 128), lambda j: (j, 0, 0)),
            pl.BlockSpec(memory_space=pl.ANY),
        ],
        out_specs=pl.BlockSpec(out_shape.shape, lambda j: (0, 0)),
        scratch_shapes=[
            pltpu.VMEM((2, 2, local_inputs, time_steps, C_BLOCK), jnp.int32),
            pltpu.SemaphoreType.DMA((2, 2)),
            pltpu.VMEM((rows, width), jnp.float32),
        ]
        + ([pltpu.VMEM((rows // 128, 2 * channels, 128), jnp.float32)] if fold_shift else []),
        compiler_params=pltpu.CompilerParams(
            dimension_semantics=("arbitrary",), vmem_limit_bytes=48 * 1024 * 1024
        ),
        cost_estimate=pl.CostEstimate(
            flops=2 * rows * 2 * NCHAN * width,
            transcendentals=0,
            bytes_accessed=voltages.size * 4 + rows * width * 4 + first.size * 4 + turn.size * 4,
        ),
    )(proto, first, turn, voltages)


def tile_coords(tile_id, blocks):
    step_row = jnp.arange(1, blocks, dtype=jnp.int32)
    triangle = step_row * (step_row + 1) // 2
    row_block = jnp.sum((tile_id[..., None] >= triangle).astype(jnp.int32), axis=-1)
    col_block = tile_id - row_block * (row_block + 1) // 2
    return (row_block, col_block)


def arrange_rows(gathered, time_steps):
    piece_count = gathered.shape[0]
    freq_count = gathered.shape[1]
    local_chans = gathered.shape[2]
    inner_width = gathered.shape[4] // time_steps
    unfolded = gathered.reshape(piece_count, freq_count, local_chans, 2, inner_width, time_steps)
    unfolded = unfolded.transpose(2, 3, 0, 5, 1, 4)
    return unfolded.reshape(local_chans, 2, piece_count * time_steps, freq_count * inner_width)


def correlate_kernel(blocks, tiles_per_step, scale, ids_ref, lhs_ref, rhs_ref, out_ref):
    step = pl.program_id(0)
    for slot in range(tiles_per_step):
        tile_id = ids_ref[step * tiles_per_step + slot]
        row_block = jnp.int32(0)
        for r in range(1, blocks):
            row_block = row_block + (tile_id >= r * (r + 1) // 2).astype(jnp.int32)
        col_block = tile_id - row_block * (row_block + 1) // 2
        rows = pl.ds(pl.multiple_of(row_block * TB, TB), TB)
        cols = pl.ds(pl.multiple_of(col_block * TB, TB), TB)
        for chan in range(lhs_ref.shape[0]):
            right = rhs_ref[chan, :, cols]
            for part in range(2):
                left = lhs_ref[chan, part, rows, :]
                product = jnp.dot(left, right, preferred_element_type=jnp.float32)
                out_ref[slot, chan, part] = product


def tile_products(spectra, tile_ids, scale):
    local_chans, depth, paths = spectra.shape
    blocks = paths // TB
    half = depth // 2
    turned_rows = spectra.transpose(0, 2, 1)
    rotated = jnp.concatenate([turned_rows[:, :, half:], -turned_rows[:, :, :half]], axis=2)
    lhs = (jnp.stack([turned_rows, rotated], axis=1) * scale).astype(spectra.dtype)
    count = tile_ids.shape[0]
    tiles_per_step = max(d for d in range(1, 10) if count % d == 0)
    kernel = lambda *refs: correlate_kernel(blocks, tiles_per_step, scale, *refs)
    out_block = (tiles_per_step, local_chans, 2, TB, TB)
    return pl.pallas_call(
        kernel,
        out_shape=jax.ShapeDtypeStruct((count, local_chans, 2, TB, TB), jnp.float32),
        grid_spec=pltpu.PrefetchScalarGridSpec(
            num_scalar_prefetch=1,
            grid=(count // tiles_per_step,),
            in_specs=[
                pl.BlockSpec(lhs.shape, lambda j, ids: (0, 0, 0, 0)),
                pl.BlockSpec(spectra.shape, lambda j, ids: (0, 0, 0)),
            ],
            out_specs=pl.BlockSpec(out_block, lambda j, ids: (j, 0, 0, 0, 0)),
        ),
        compiler_params=pltpu.CompilerParams(
            dimension_semantics=("arbitrary",), vmem_limit_bytes=48 * 1024 * 1024
        ),
        cost_estimate=pl.CostEstimate(
            flops=2 * count * local_chans * 2 * TB * TB * depth,
            transcendentals=0,
            bytes_accessed=count * local_chans * 2 * TB * TB * 4 + lhs.size * 2 + spectra.size * 2,
        ),
    )(tile_ids, lhs, spectra)


def on_device(voltages, tile_map):
    local_inputs = voltages.shape[0]
    time_steps = voltages.shape[1]
    freq_devices = lax.axis_size("freq")
    time_devices = lax.axis_size("tm")
    channels = CH_DEV * freq_devices
    first_channel = NCHAN // 2 - channels // 2
    proto = prototype_rows()
    first, turn = phase_tables(first_channel, channels)
    if time_devices == 1:
        spectra = tap_products(voltages, proto, first, turn, channels, True)
    else:
        products = tap_products(voltages, proto, first, turn, channels, False)
        products = products.reshape(local_inputs, time_steps, TAPS, 2 * channels)
        tail = products[:, time_steps - (TAPS - 1) :]
        previous = passed_along(tail, "tm", 1)
        total = None
        for tap in range(TAPS):
            lead = TAPS - 1 - tap
            shifted = jnp.concatenate(
                [previous[:, tap:, tap], products[:, : time_steps - lead, tap]], axis=1
            )
            total = shifted if total is None else total + shifted
        spectra = total.reshape(local_inputs * time_steps, 2, channels).transpose(2, 1, 0)
        spectra = spectra.astype(jnp.bfloat16)
    spectra = spectra.reshape(freq_devices, CH_DEV, 2, local_inputs * time_steps)
    turned = lax.all_to_all(spectra, "freq", split_axis=0, concat_axis=0, tiled=True)
    slot_count = tile_map.shape[0] // time_devices
    inverse_count = 1.0 / (time_steps * time_devices)
    tile_ids = lax.dynamic_slice_in_dim(tile_map, lax.axis_index("tm") * slot_count, slot_count)
    arranged = arrange_rows(lax.all_gather(turned[None], "tm", axis=0, tiled=True), time_steps)
    arranged = arranged.reshape(arranged.shape[0], -1, arranged.shape[3])
    return tile_products(arranged, tile_ids, inverse_count)


def solution(mesh):
    in_specs = (P("freq", "tm", None, None), P())
    out_specs = P("tm", "freq", None, None, None)
    return jax.shard_map(
        on_device, mesh=mesh, in_specs=in_specs, out_specs=out_specs, check_vma=False
    )
```

```python
import math

import jax
import jax.numpy as jnp
from jax import lax
from jax.experimental import pallas as pl
from jax.experimental.pallas import tpu as pltpu
from jax.sharding import PartitionSpec as P

NCHAN = 4096
TAPS = 4
TB = 128
CH_DEV = 2
C_BLOCK = 1024
LANES = 128


def passed_along(value, axis, steps):
    count = lax.axis_size(axis)
    leading, last = (max(0, -steps), min(count, count - steps))
    return lax.ppermute(value, axis, [(source, source + steps) for source in range(leading, last)])


def prototype_rows():
    sample_idx = jnp.arange(TAPS * NCHAN, dtype=jnp.int32)
    position = (sample_idx.astype(jnp.float32) + 0.5) / NCHAN - TAPS / 2.0
    hann_taper = 0.5 - 0.5 * jnp.cos(
        (sample_idx.astype(jnp.float32) + 0.5) * (2.0 * math.pi / (TAPS * NCHAN))
    )
    return (jnp.sinc(position) * hann_taper / (128.0 * math.sqrt(NCHAN))).reshape(TAPS, NCHAN)


def phase_tables(first_channel, channels):
    channel = first_channel + jnp.arange(channels, dtype=jnp.int32)
    step = 2.0 * math.pi / NCHAN
    lane = jnp.arange(LANES, dtype=jnp.int32)
    start = ((lane[None, :] * channel[:, None]) % NCHAN).astype(jnp.float32) * step
    first = jnp.concatenate([jnp.cos(start), jnp.sin(start)], axis=0)
    chunk = jnp.arange(NCHAN // LANES, dtype=jnp.int32) * LANES
    shift = ((chunk[:, None] * channel[None, :]) % NCHAN).astype(jnp.float32) * step
    return first, jnp.concatenate([jnp.cos(shift), jnp.sin(shift)], axis=1)


def channelize_kernel(
    channels, fold_shift, proto_ref, first_ref, turn_ref, x_hbm, out_ref, buf, sems, acc_ref, *scratch
):
    step = pl.program_id(0)
    count = pl.num_programs(0)
    cb = buf.shape[-1]

    def fetch(block, slot):
        for part in range(2):
            pltpu.make_async_copy(
                x_hbm.at[:, :, part, pl.ds(block * cb, cb)], buf.at[slot, part], sems.at[slot, part]
            ).start()

    @pl.when(step == 0)
    def _():
        fetch(0, 0)

    @pl.when(step + 1 < count)
    def _():
        fetch(step + 1, (step + 1) % 2)

    slot = step % 2
    for part in range(2):
        pltpu.make_async_copy(
            x_hbm.at[:, :, part, pl.ds(0, cb)], buf.at[slot, part], sems.at[slot, part]
        ).wait()
    turn = turn_ref[...].T
    cos_0, sin_0 = first_ref[:channels], first_ref[channels:]
    cos_parts, sin_parts = [], []
    for chunk in range(cb // LANES):
        cos_t = jnp.broadcast_to(turn[:channels, chunk : chunk + 1], cos_0.shape)
        sin_t = jnp.broadcast_to(turn[channels:, chunk : chunk + 1], cos_0.shape)
        cos_parts.append(cos_0 * cos_t - sin_0 * sin_t)
        sin_parts.append(sin_0 * cos_t + cos_0 * sin_t)
    cosine = jnp.concatenate(cos_parts, axis=1)
    sine = jnp.concatenate(sin_parts, axis=1)
    upper = jnp.concatenate([cosine, -sine], axis=0)
    lower = jnp.concatenate([sine, cosine], axis=0)
    weights = proto_ref[...]
    re_tables = []
    im_tables = []
    for tap in range(TAPS):
        w = weights[tap : tap + 1, :]
        re_tables.append((w * upper).astype(jnp.bfloat16))
        im_tables.append((w * lower).astype(jnp.bfloat16))
    re_table = jnp.concatenate(re_tables, axis=0)
    im_table = jnp.concatenate(im_tables, axis=0)
    rows = buf.shape[2] * buf.shape[3]
    x_re = buf[slot, 0].reshape(rows, cb).astype(jnp.bfloat16)
    x_im = buf[slot, 1].reshape(rows, cb).astype(jnp.bfloat16)
    dims = (((1,), (1,)), ((), ()))
    part = lax.dot_general(x_re, re_table, dims, preferred_element_type=jnp.float32) + lax.dot_general(
        x_im, im_table, dims, preferred_element_type=jnp.float32
    )

    @pl.when(step == 0)
    def _():
        acc_ref[...] = part

    @pl.when(jnp.logical_and(step > 0, step < count - 1))
    def _():
        acc_ref[...] += part

    @pl.when(step == count - 1)
    def _():
        products = acc_ref[...] + part
        if not fold_shift:
            out_ref[...] = products
            return
        time_steps = buf.shape[3]
        width = 2 * channels
        block = lax.broadcasted_iota(jnp.int32, (rows, width), 0) % time_steps
        total = None
        for tap in range(TAPS):
            term = products[:, tap * width : (tap + 1) * width]
            lead = TAPS - 1 - tap
            if lead:
                term = jnp.where(block >= lead, pltpu.roll(term, lead, 0), 0.0)
            total = term if total is None else total + term
        (staged,) = scratch
        lanes = staged.shape[-1]
        for half in range(2):
            rows_q = pl.ds(half, channels, stride=2)
            flipped = total[:, half * channels : (half + 1) * channels].T
            for chunk in range(staged.shape[0]):
                staged[chunk, rows_q, :] = flipped[:, chunk * lanes : (chunk + 1) * lanes]
        for chunk in range(staged.shape[0]):
            out_ref[:, chunk * lanes : (chunk + 1) * lanes] = staged[chunk].astype(out_ref.dtype)


def tap_products(voltages, proto, first, turn, channels, fold_shift):
    local_inputs, time_steps = voltages.shape[0], voltages.shape[1]
    rows = local_inputs * time_steps
    width = TAPS * 2 * channels
    blocks = NCHAN // C_BLOCK
    kernel = lambda *refs: channelize_kernel(channels, fold_shift, *refs)
    if fold_shift:
        out_shape = jax.ShapeDtypeStruct((2 * channels, rows), jnp.bfloat16)
    else:
        out_shape = jax.ShapeDtypeStruct((rows, width), jnp.float32)
    return pl.pallas_call(
        kernel,
        out_shape=out_shape,
        grid=(blocks,),
        in_specs=[
            pl.BlockSpec((TAPS, C_BLOCK), lambda j: (0, j)),
            pl.BlockSpec((2 * channels, LANES), lambda j: (0, 0)),
            pl.BlockSpec((C_BLOCK // LANES, 2 * channels), lambda j: (j, 0)),
            pl.BlockSpec(memory_space=pl.ANY),
        ],
        out_specs=pl.BlockSpec(out_shape.shape, lambda j: (0, 0)),
        scratch_shapes=[
            pltpu.VMEM((2, 2, local_inputs, time_steps, C_BLOCK), jnp.int32),
            pltpu.SemaphoreType.DMA((2, 2)),
            pltpu.VMEM((rows, width), jnp.float32),
        ]
        + ([pltpu.VMEM((rows // 128, 2 * channels, 128), jnp.float32)] if fold_shift else []),
        compiler_params=pltpu.CompilerParams(
            dimension_semantics=("arbitrary",), vmem_limit_bytes=48 * 1024 * 1024
        ),
        cost_estimate=pl.CostEstimate(
            flops=2 * rows * 2 * NCHAN * width,
            transcendentals=0,
            bytes_accessed=voltages.size * 4 + rows * width * 4 + first.size * 4 + turn.size * 4,
        ),
    )(proto, first, turn, voltages)


def tile_coords(tile_id, blocks):
    step_row = jnp.arange(1, blocks, dtype=jnp.int32)
    triangle = step_row * (step_row + 1) // 2
    row_block = jnp.sum((tile_id[..., None] >= triangle).astype(jnp.int32), axis=-1)
    col_block = tile_id - row_block * (row_block + 1) // 2
    return (row_block, col_block)


def arrange_rows(gathered, time_steps):
    piece_count = gathered.shape[0]
    freq_count = gathered.shape[1]
    local_chans = gathered.shape[2]
    inner_width = gathered.shape[4] // time_steps
    unfolded = gathered.reshape(piece_count, freq_count, local_chans, 2, inner_width, time_steps)
    unfolded = unfolded.transpose(2, 3, 0, 5, 1, 4)
    return unfolded.reshape(local_chans, 2, piece_count * time_steps, freq_count * inner_width)


def correlate_kernel(blocks, tiles_per_step, scale, ids_ref, lhs_ref, rhs_ref, out_ref):
    step = pl.program_id(0)
    for slot in range(tiles_per_step):
        tile_id = ids_ref[step * tiles_per_step + slot]
        row_block = jnp.int32(0)
        for r in range(1, blocks):
            row_block = row_block + (tile_id >= r * (r + 1) // 2).astype(jnp.int32)
        col_block = tile_id - row_block * (row_block + 1) // 2
        rows = pl.ds(pl.multiple_of(row_block * TB, TB), TB)
        cols = pl.ds(pl.multiple_of(col_block * TB, TB), TB)
        for chan in range(lhs_ref.shape[0]):
            right = rhs_ref[chan, :, cols]
            for part in range(2):
                left = lhs_ref[chan, part, rows, :]
                product = jnp.dot(left, right, preferred_element_type=jnp.float32)
                out_ref[slot, chan, part] = product


def tile_products(spectra, tile_ids, scale):
    local_chans, depth, paths = spectra.shape
    blocks = paths // TB
    half = depth // 2
    turned_rows = spectra.transpose(0, 2, 1)
    rotated = jnp.concatenate([turned_rows[:, :, half:], -turned_rows[:, :, :half]], axis=2)
    lhs = (jnp.stack([turned_rows, rotated], axis=1) * scale).astype(spectra.dtype)
    count = tile_ids.shape[0]
    tiles_per_step = max(d for d in range(1, 10) if count % d == 0)
    kernel = lambda *refs: correlate_kernel(blocks, tiles_per_step, scale, *refs)
    out_block = (tiles_per_step, local_chans, 2, TB, TB)
    return pl.pallas_call(
        kernel,
        out_shape=jax.ShapeDtypeStruct((count, local_chans, 2, TB, TB), jnp.float32),
        grid_spec=pltpu.PrefetchScalarGridSpec(
            num_scalar_prefetch=1,
            grid=(count // tiles_per_step,),
            in_specs=[
                pl.BlockSpec(lhs.shape, lambda j, ids: (0, 0, 0, 0)),
                pl.BlockSpec(spectra.shape, lambda j, ids: (0, 0, 0)),
            ],
            out_specs=pl.BlockSpec(out_block, lambda j, ids: (j, 0, 0, 0, 0)),
        ),
        compiler_params=pltpu.CompilerParams(
            dimension_semantics=("arbitrary",), vmem_limit_bytes=48 * 1024 * 1024
        ),
        cost_estimate=pl.CostEstimate(
            flops=2 * count * local_chans * 2 * TB * TB * depth,
            transcendentals=0,
            bytes_accessed=count * local_chans * 2 * TB * TB * 4 + lhs.size * 2 + spectra.size * 2,
        ),
    )(tile_ids, lhs, spectra)


def on_device(voltages, tile_map):
    local_inputs = voltages.shape[0]
    time_steps = voltages.shape[1]
    freq_devices = lax.axis_size("freq")
    time_devices = lax.axis_size("tm")
    channels = CH_DEV * freq_devices
    first_channel = NCHAN // 2 - channels // 2
    proto = prototype_rows()
    first, turn = phase_tables(first_channel, channels)
    if time_devices == 1:
        spectra = tap_products(voltages, proto, first, turn, channels, True)
    else:
        products = tap_products(voltages, proto, first, turn, channels, False)
        products = products.reshape(local_inputs, time_steps, TAPS, 2 * channels)
        tail = products[:, time_steps - (TAPS - 1) :]
        previous = passed_along(tail, "tm", 1)
        total = None
        for tap in range(TAPS):
            lead = TAPS - 1 - tap
            shifted = jnp.concatenate(
                [previous[:, tap:, tap], products[:, : time_steps - lead, tap]], axis=1
            )
            total = shifted if total is None else total + shifted
        spectra = total.reshape(local_inputs * time_steps, 2, channels).transpose(2, 1, 0)
        spectra = spectra.astype(jnp.bfloat16)
    spectra = spectra.reshape(freq_devices, CH_DEV, 2, local_inputs * time_steps)
    turned = lax.all_to_all(spectra, "freq", split_axis=0, concat_axis=0, tiled=True)
    slot_count = tile_map.shape[0] // time_devices
    inverse_count = 1.0 / (time_steps * time_devices)
    tile_ids = lax.dynamic_slice_in_dim(tile_map, lax.axis_index("tm") * slot_count, slot_count)
    arranged = arrange_rows(lax.all_gather(turned[None], "tm", axis=0, tiled=True), time_steps)
    arranged = arranged.reshape(arranged.shape[0], -1, arranged.shape[3])
    return tile_products(arranged, tile_ids, inverse_count)


def solution(mesh):
    in_specs = (P("freq", "tm", None, None), P())
    out_specs = P("tm", "freq", None, None, None)
    return jax.shard_map(
        on_device, mesh=mesh, in_specs=in_specs, out_specs=out_specs, check_vma=False
    )
```

```python
import math

import jax
import jax.numpy as jnp
from jax import lax
from jax.experimental import pallas as pl
from jax.experimental.pallas import tpu as pltpu
from jax.sharding import PartitionSpec as P

NCHAN = 4096
TAPS = 4
TB = 128
CH_DEV = 2
C_BLOCK = 1024
LANES = 128


def passed_along(value, axis, steps):
    count = lax.axis_size(axis)
    leading, last = (max(0, -steps), min(count, count - steps))
    return lax.ppermute(value, axis, [(source, source + steps) for source in range(leading, last)])


def prototype_rows():
    sample_idx = jnp.arange(TAPS * NCHAN, dtype=jnp.int32)
    position = (sample_idx.astype(jnp.float32) + 0.5) / NCHAN - TAPS / 2.0
    hann_taper = 0.5 - 0.5 * jnp.cos(
        (sample_idx.astype(jnp.float32) + 0.5) * (2.0 * math.pi / (TAPS * NCHAN))
    )
    return (jnp.sinc(position) * hann_taper / (128.0 * math.sqrt(NCHAN))).reshape(TAPS, NCHAN)


def phase_tables(first_channel, channels):
    channel = first_channel + jnp.arange(channels, dtype=jnp.int32)
    step = 2.0 * math.pi / NCHAN
    lane = jnp.arange(LANES, dtype=jnp.int32)
    start = ((lane[None, :] * channel[:, None]) % NCHAN).astype(jnp.float32) * step
    first = jnp.concatenate([jnp.cos(start), jnp.sin(start)], axis=0)
    chunk = jnp.arange(NCHAN // LANES, dtype=jnp.int32) * LANES
    shift = ((chunk[:, None] * channel[None, :]) % NCHAN).astype(jnp.float32) * step
    return first, jnp.concatenate([jnp.cos(shift), jnp.sin(shift)], axis=1)


def channelize_kernel(
    channels, fold_shift, proto_ref, first_ref, turn_ref, x_hbm, out_ref, buf, sems, acc_ref, *scratch
):
    step = pl.program_id(0)
    count = pl.num_programs(0)
    cb = buf.shape[-1]

    def fetch(block, slot):
        for part in range(2):
            pltpu.make_async_copy(
                x_hbm.at[:, :, part, pl.ds(block * cb, cb)], buf.at[slot, part], sems.at[slot, part]
            ).start()

    @pl.when(step == 0)
    def _():
        fetch(0, 0)

    @pl.when(step + 1 < count)
    def _():
        fetch(step + 1, (step + 1) % 2)

    slot = step % 2
    for part in range(2):
        pltpu.make_async_copy(
            x_hbm.at[:, :, part, pl.ds(0, cb)], buf.at[slot, part], sems.at[slot, part]
        ).wait()
    turn = turn_ref[...].T
    cos_0, sin_0 = first_ref[:channels], first_ref[channels:]
    cos_parts, sin_parts = [], []
    for chunk in range(cb // LANES):
        cos_t = jnp.broadcast_to(turn[:channels, chunk : chunk + 1], cos_0.shape)
        sin_t = jnp.broadcast_to(turn[channels:, chunk : chunk + 1], cos_0.shape)
        cos_parts.append(cos_0 * cos_t - sin_0 * sin_t)
        sin_parts.append(sin_0 * cos_t + cos_0 * sin_t)
    cosine = jnp.concatenate(cos_parts, axis=1)
    sine = jnp.concatenate(sin_parts, axis=1)
    upper = jnp.concatenate([cosine, -sine], axis=0)
    lower = jnp.concatenate([sine, cosine], axis=0)
    weights = proto_ref[...]
    re_tables = []
    im_tables = []
    for tap in range(TAPS):
        w = weights[tap : tap + 1, :]
        re_tables.append((w * upper).astype(jnp.bfloat16))
        im_tables.append((w * lower).astype(jnp.bfloat16))
    re_table = jnp.concatenate(re_tables, axis=0)
    im_table = jnp.concatenate(im_tables, axis=0)
    rows = buf.shape[2] * buf.shape[3]
    x_re = buf[slot, 0].reshape(rows, cb).astype(jnp.bfloat16)
    x_im = buf[slot, 1].reshape(rows, cb).astype(jnp.bfloat16)
    dims = (((1,), (1,)), ((), ()))
    part = lax.dot_general(x_re, re_table, dims, preferred_element_type=jnp.float32) + lax.dot_general(
        x_im, im_table, dims, preferred_element_type=jnp.float32
    )

    @pl.when(step == 0)
    def _():
        acc_ref[...] = part

    @pl.when(jnp.logical_and(step > 0, step < count - 1))
    def _():
        acc_ref[...] += part

    @pl.when(step == count - 1)
    def _():
        products = acc_ref[...] + part
        if not fold_shift:
            out_ref[...] = products
            return
        time_steps = buf.shape[3]
        width = 2 * channels
        block = lax.broadcasted_iota(jnp.int32, (rows, width), 0) % time_steps
        total = None
        for tap in range(TAPS):
            term = products[:, tap * width : (tap + 1) * width]
            lead = TAPS - 1 - tap
            if lead:
                term = jnp.where(block >= lead, pltpu.roll(term, lead, 0), 0.0)
            total = term if total is None else total + term
        (staged,) = scratch
        lanes = staged.shape[-1]
        for half in range(2):
            rows_q = pl.ds(half, channels, stride=2)
            flipped = total[:, half * channels : (half + 1) * channels].T
            for chunk in range(staged.shape[0]):
                staged[chunk, rows_q, :] = flipped[:, chunk * lanes : (chunk + 1) * lanes]
        for chunk in range(staged.shape[0]):
            out_ref[:, chunk * lanes : (chunk + 1) * lanes] = staged[chunk].astype(out_ref.dtype)


def tap_products(voltages, proto, first, turn, channels, fold_shift):
    local_inputs, time_steps = voltages.shape[0], voltages.shape[1]
    rows = local_inputs * time_steps
    width = TAPS * 2 * channels
    blocks = NCHAN // C_BLOCK
    kernel = lambda *refs: channelize_kernel(channels, fold_shift, *refs)
    if fold_shift:
        out_shape = jax.ShapeDtypeStruct((2 * channels, rows), jnp.bfloat16)
    else:
        out_shape = jax.ShapeDtypeStruct((rows, width), jnp.float32)
    return pl.pallas_call(
        kernel,
        out_shape=out_shape,
        grid=(blocks,),
        in_specs=[
            pl.BlockSpec((TAPS, C_BLOCK), lambda j: (0, j)),
            pl.BlockSpec((2 * channels, LANES), lambda j: (0, 0)),
            pl.BlockSpec((C_BLOCK // LANES, 2 * channels), lambda j: (j, 0)),
            pl.BlockSpec(memory_space=pl.ANY),
        ],
        out_specs=pl.BlockSpec(out_shape.shape, lambda j: (0, 0)),
        scratch_shapes=[
            pltpu.VMEM((2, 2, local_inputs, time_steps, C_BLOCK), jnp.int32),
            pltpu.SemaphoreType.DMA((2, 2)),
            pltpu.VMEM((rows, width), jnp.float32),
        ]
        + ([pltpu.VMEM((rows // 128, 2 * channels, 128), jnp.float32)] if fold_shift else []),
        compiler_params=pltpu.CompilerParams(
            dimension_semantics=("arbitrary",), vmem_limit_bytes=48 * 1024 * 1024
        ),
        cost_estimate=pl.CostEstimate(
            flops=2 * rows * 2 * NCHAN * width,
            transcendentals=0,
            bytes_accessed=voltages.size * 4 + rows * width * 4 + first.size * 4 + turn.size * 4,
        ),
    )(proto, first, turn, voltages)


def tile_coords(tile_id, blocks):
    step_row = jnp.arange(1, blocks, dtype=jnp.int32)
    triangle = step_row * (step_row + 1) // 2
    row_block = jnp.sum((tile_id[..., None] >= triangle).astype(jnp.int32), axis=-1)
    col_block = tile_id - row_block * (row_block + 1) // 2
    return (row_block, col_block)


def arrange_rows(gathered, time_steps):
    piece_count = gathered.shape[0]
    freq_count = gathered.shape[1]
    local_chans = gathered.shape[2]
    inner_width = gathered.shape[4] // time_steps
    unfolded = gathered.reshape(piece_count, freq_count, local_chans, 2, inner_width, time_steps)
    unfolded = unfolded.transpose(2, 3, 0, 5, 1, 4)
    return unfolded.reshape(local_chans, 2, piece_count * time_steps, freq_count * inner_width)


def correlate_kernel(blocks, groups, ids_ref, lhs_ref, rhs_ref, out_hbm, staged, sems):
    count = staged.shape[0]
    per_group = count // groups

    def copy(group):
        part = pl.ds(group * per_group, per_group)
        return pltpu.make_async_copy(staged.at[part], out_hbm.at[part], sems.at[group])

    for group in range(groups):
        for slot in range(group * per_group, (group + 1) * per_group):
            tile_id = ids_ref[slot]
            row_block = jnp.int32(0)
            for r in range(1, blocks):
                row_block = row_block + (tile_id >= r * (r + 1) // 2).astype(jnp.int32)
            col_block = tile_id - row_block * (row_block + 1) // 2
            rows = pl.ds(pl.multiple_of(row_block * TB, TB), TB)
            cols = pl.ds(pl.multiple_of(col_block * TB, TB), TB)
            for chan in range(lhs_ref.shape[0]):
                right = rhs_ref[chan, :, cols]
                for part in range(2):
                    left = lhs_ref[chan, part, rows, :]
                    staged[slot, chan, part] = jnp.dot(left, right, preferred_element_type=jnp.float32)
        copy(group).start()
    for group in range(groups):
        copy(group).wait()


def tile_products(spectra, tile_ids, scale):
    local_chans, depth, paths = spectra.shape
    blocks = paths // TB
    half = depth // 2
    turned_rows = spectra.transpose(0, 2, 1)
    rotated = jnp.concatenate([turned_rows[:, :, half:], -turned_rows[:, :, :half]], axis=2)
    lhs = (jnp.stack([turned_rows, rotated], axis=1) * scale).astype(spectra.dtype)
    count = tile_ids.shape[0]
    groups = max(d for d in range(1, 5) if count % d == 0)
    kernel = lambda *refs: correlate_kernel(blocks, groups, *refs)
    out_shape = (count, local_chans, 2, TB, TB)
    return pl.pallas_call(
        kernel,
        out_shape=jax.ShapeDtypeStruct(out_shape, jnp.float32),
        in_specs=[
            pl.BlockSpec(memory_space=pltpu.SMEM),
            pl.BlockSpec(memory_space=pltpu.VMEM),
            pl.BlockSpec(memory_space=pltpu.VMEM),
        ],
        out_specs=pl.BlockSpec(memory_space=pl.ANY),
        scratch_shapes=[pltpu.VMEM(out_shape, jnp.float32), pltpu.SemaphoreType.DMA((groups,))],
        compiler_params=pltpu.CompilerParams(vmem_limit_bytes=48 * 1024 * 1024),
        cost_estimate=pl.CostEstimate(
            flops=2 * count * local_chans * 2 * TB * TB * depth,
            transcendentals=0,
            bytes_accessed=count * local_chans * 2 * TB * TB * 4 + lhs.size * 2 + spectra.size * 2,
        ),
    )(tile_ids, lhs, spectra)


def on_device(voltages, tile_map):
    local_inputs = voltages.shape[0]
    time_steps = voltages.shape[1]
    freq_devices = lax.axis_size("freq")
    time_devices = lax.axis_size("tm")
    channels = CH_DEV * freq_devices
    first_channel = NCHAN // 2 - channels // 2
    proto = prototype_rows()
    first, turn = phase_tables(first_channel, channels)
    if time_devices == 1:
        spectra = tap_products(voltages, proto, first, turn, channels, True)
    else:
        products = tap_products(voltages, proto, first, turn, channels, False)
        products = products.reshape(local_inputs, time_steps, TAPS, 2 * channels)
        tail = products[:, time_steps - (TAPS - 1) :]
        previous = passed_along(tail, "tm", 1)
        total = None
        for tap in range(TAPS):
            lead = TAPS - 1 - tap
            shifted = jnp.concatenate(
                [previous[:, tap:, tap], products[:, : time_steps - lead, tap]], axis=1
            )
            total = shifted if total is None else total + shifted
        spectra = total.reshape(local_inputs * time_steps, 2, channels).transpose(2, 1, 0)
        spectra = spectra.astype(jnp.bfloat16)
    spectra = spectra.reshape(freq_devices, CH_DEV, 2, local_inputs * time_steps)
    turned = lax.all_to_all(spectra, "freq", split_axis=0, concat_axis=0, tiled=True)
    slot_count = tile_map.shape[0] // time_devices
    inverse_count = 1.0 / (time_steps * time_devices)
    tile_ids = lax.dynamic_slice_in_dim(tile_map, lax.axis_index("tm") * slot_count, slot_count)
    arranged = arrange_rows(lax.all_gather(turned[None], "tm", axis=0, tiled=True), time_steps)
    arranged = arranged.reshape(arranged.shape[0], -1, arranged.shape[3])
    return tile_products(arranged, tile_ids, inverse_count)


def solution(mesh):
    in_specs = (P("freq", "tm", None, None), P())
    out_specs = P("tm", "freq", None, None, None)
    return jax.shard_map(
        on_device, mesh=mesh, in_specs=in_specs, out_specs=out_specs, check_vma=False
    )
```

```python
import math

import jax
import jax.numpy as jnp
from jax import lax
from jax.experimental import pallas as pl
from jax.experimental.pallas import tpu as pltpu
from jax.sharding import PartitionSpec as P

NCHAN = 4096
TAPS = 4
TB = 128
CH_DEV = 2
C_BLOCK = 2048
LANES = 128


def passed_along(value, axis, steps):
    count = lax.axis_size(axis)
    leading, last = (max(0, -steps), min(count, count - steps))
    return lax.ppermute(value, axis, [(source, source + steps) for source in range(leading, last)])


def prototype_rows():
    sample_idx = jnp.arange(TAPS * NCHAN, dtype=jnp.int32)
    position = (sample_idx.astype(jnp.float32) + 0.5) / NCHAN - TAPS / 2.0
    hann_taper = 0.5 - 0.5 * jnp.cos(
        (sample_idx.astype(jnp.float32) + 0.5) * (2.0 * math.pi / (TAPS * NCHAN))
    )
    return (jnp.sinc(position) * hann_taper / (128.0 * math.sqrt(NCHAN))).reshape(TAPS, NCHAN)


def phase_tables(first_channel, channels):
    channel = first_channel + jnp.arange(channels, dtype=jnp.int32)
    step = 2.0 * math.pi / NCHAN
    lane = jnp.arange(LANES, dtype=jnp.int32)
    start = ((lane[None, :] * channel[:, None]) % NCHAN).astype(jnp.float32) * step
    first = jnp.concatenate([jnp.cos(start), jnp.sin(start)], axis=0)
    chunk = jnp.arange(NCHAN // LANES, dtype=jnp.int32) * LANES
    shift = ((chunk[:, None] * channel[None, :]) % NCHAN).astype(jnp.float32) * step
    return first, jnp.concatenate([jnp.cos(shift), jnp.sin(shift)], axis=1)


def channelize_kernel(
    channels, fold_shift, proto_ref, first_ref, turn_ref, x_hbm, out_ref, buf, sems, acc_ref, *scratch
):
    step = pl.program_id(0)
    count = pl.num_programs(0)
    cb = buf.shape[-1]

    def fetch(block, slot):
        for part in range(2):
            pltpu.make_async_copy(
                x_hbm.at[:, :, part, pl.ds(block * cb, cb)], buf.at[slot, part], sems.at[slot, part]
            ).start()

    @pl.when(step == 0)
    def _():
        fetch(0, 0)

    @pl.when(step + 1 < count)
    def _():
        fetch(step + 1, (step + 1) % 2)

    slot = step % 2
    for part in range(2):
        pltpu.make_async_copy(
            x_hbm.at[:, :, part, pl.ds(0, cb)], buf.at[slot, part], sems.at[slot, part]
        ).wait()
    turn = turn_ref[...].T
    cos_0, sin_0 = first_ref[:channels], first_ref[channels:]
    cos_parts, sin_parts = [], []
    for chunk in range(cb // LANES):
        cos_t = jnp.broadcast_to(turn[:channels, chunk : chunk + 1], cos_0.shape)
        sin_t = jnp.broadcast_to(turn[channels:, chunk : chunk + 1], cos_0.shape)
        cos_parts.append(cos_0 * cos_t - sin_0 * sin_t)
        sin_parts.append(sin_0 * cos_t + cos_0 * sin_t)
    cosine = jnp.concatenate(cos_parts, axis=1)
    sine = jnp.concatenate(sin_parts, axis=1)
    upper = jnp.concatenate([cosine, -sine], axis=0)
    lower = jnp.concatenate([sine, cosine], axis=0)
    weights = proto_ref[...]
    re_tables = []
    im_tables = []
    for tap in range(TAPS):
        w = weights[tap : tap + 1, :]
        re_tables.append((w * upper).astype(jnp.bfloat16))
        im_tables.append((w * lower).astype(jnp.bfloat16))
    re_table = jnp.concatenate(re_tables, axis=0)
    im_table = jnp.concatenate(im_tables, axis=0)
    rows = buf.shape[2] * buf.shape[3]
    x_re = buf[slot, 0].reshape(rows, cb).astype(jnp.bfloat16)
    x_im = buf[slot, 1].reshape(rows, cb).astype(jnp.bfloat16)
    dims = (((1,), (1,)), ((), ()))
    part = lax.dot_general(x_re, re_table, dims, preferred_element_type=jnp.float32) + lax.dot_general(
        x_im, im_table, dims, preferred_element_type=jnp.float32
    )

    @pl.when(step == 0)
    def _():
        acc_ref[...] = part

    @pl.when(jnp.logical_and(step > 0, step < count - 1))
    def _():
        acc_ref[...] += part

    @pl.when(step == count - 1)
    def _():
        products = acc_ref[...] + part
        if not fold_shift:
            out_ref[...] = products
            return
        time_steps = buf.shape[3]
        width = 2 * channels
        block = lax.broadcasted_iota(jnp.int32, (rows, width), 0) % time_steps
        total = None
        for tap in range(TAPS):
            term = products[:, tap * width : (tap + 1) * width]
            lead = TAPS - 1 - tap
            if lead:
                term = jnp.where(block >= lead, pltpu.roll(term, lead, 0), 0.0)
            total = term if total is None else total + term
        (staged,) = scratch
        lanes = staged.shape[-1]
        for half in range(2):
            rows_q = pl.ds(half, channels, stride=2)
            flipped = total[:, half * channels : (half + 1) * channels].T
            for chunk in range(staged.shape[0]):
                staged[chunk, rows_q, :] = flipped[:, chunk * lanes : (chunk + 1) * lanes]
        for chunk in range(staged.shape[0]):
            out_ref[:, chunk * lanes : (chunk + 1) * lanes] = staged[chunk].astype(out_ref.dtype)


def tap_products(voltages, proto, first, turn, channels, fold_shift):
    local_inputs, time_steps = voltages.shape[0], voltages.shape[1]
    rows = local_inputs * time_steps
    width = TAPS * 2 * channels
    blocks = NCHAN // C_BLOCK
    kernel = lambda *refs: channelize_kernel(channels, fold_shift, *refs)
    if fold_shift:
        out_shape = jax.ShapeDtypeStruct((2 * channels, rows), jnp.bfloat16)
    else:
        out_shape = jax.ShapeDtypeStruct((rows, width), jnp.float32)
    return pl.pallas_call(
        kernel,
        out_shape=out_shape,
        grid=(blocks,),
        in_specs=[
            pl.BlockSpec((TAPS, C_BLOCK), lambda j: (0, j)),
            pl.BlockSpec((2 * channels, LANES), lambda j: (0, 0)),
            pl.BlockSpec((C_BLOCK // LANES, 2 * channels), lambda j: (j, 0)),
            pl.BlockSpec(memory_space=pl.ANY),
        ],
        out_specs=pl.BlockSpec(out_shape.shape, lambda j: (0, 0)),
        scratch_shapes=[
            pltpu.VMEM((2, 2, local_inputs, time_steps, C_BLOCK), jnp.int32),
            pltpu.SemaphoreType.DMA((2, 2)),
            pltpu.VMEM((rows, width), jnp.float32),
        ]
        + ([pltpu.VMEM((rows // 128, 2 * channels, 128), jnp.float32)] if fold_shift else []),
        compiler_params=pltpu.CompilerParams(
            dimension_semantics=("arbitrary",), vmem_limit_bytes=48 * 1024 * 1024
        ),
        cost_estimate=pl.CostEstimate(
            flops=2 * rows * 2 * NCHAN * width,
            transcendentals=0,
            bytes_accessed=voltages.size * 4 + rows * width * 4 + first.size * 4 + turn.size * 4,
        ),
    )(proto, first, turn, voltages)


def tile_coords(tile_id, blocks):
    step_row = jnp.arange(1, blocks, dtype=jnp.int32)
    triangle = step_row * (step_row + 1) // 2
    row_block = jnp.sum((tile_id[..., None] >= triangle).astype(jnp.int32), axis=-1)
    col_block = tile_id - row_block * (row_block + 1) // 2
    return (row_block, col_block)


def arrange_rows(gathered, time_steps):
    piece_count = gathered.shape[0]
    freq_count = gathered.shape[1]
    local_chans = gathered.shape[2]
    inner_width = gathered.shape[4] // time_steps
    unfolded = gathered.reshape(piece_count, freq_count, local_chans, 2, inner_width, time_steps)
    unfolded = unfolded.transpose(2, 3, 0, 5, 1, 4)
    return unfolded.reshape(local_chans, 2, piece_count * time_steps, freq_count * inner_width)


def correlate_kernel(blocks, groups, ids_ref, lhs_ref, rhs_ref, out_hbm, staged, sems):
    count = staged.shape[0]
    per_group = count // groups

    def copy(group):
        part = pl.ds(group * per_group, per_group)
        return pltpu.make_async_copy(staged.at[part], out_hbm.at[part], sems.at[group])

    for group in range(groups):
        for slot in range(group * per_group, (group + 1) * per_group):
            tile_id = ids_ref[slot]
            row_block = jnp.int32(0)
            for r in range(1, blocks):
                row_block = row_block + (tile_id >= r * (r + 1) // 2).astype(jnp.int32)
            col_block = tile_id - row_block * (row_block + 1) // 2
            rows = pl.ds(pl.multiple_of(row_block * TB, TB), TB)
            cols = pl.ds(pl.multiple_of(col_block * TB, TB), TB)
            for chan in range(lhs_ref.shape[0]):
                right = rhs_ref[chan, :, cols]
                for part in range(2):
                    left = lhs_ref[chan, part, rows, :]
                    staged[slot, chan, part] = jnp.dot(left, right, preferred_element_type=jnp.float32)
        copy(group).start()
    for group in range(groups):
        copy(group).wait()


def tile_products(spectra, tile_ids, scale):
    local_chans, depth, paths = spectra.shape
    blocks = paths // TB
    half = depth // 2
    turned_rows = spectra.transpose(0, 2, 1)
    rotated = jnp.concatenate([turned_rows[:, :, half:], -turned_rows[:, :, :half]], axis=2)
    lhs = (jnp.stack([turned_rows, rotated], axis=1) * scale).astype(spectra.dtype)
    count = tile_ids.shape[0]
    groups = max(d for d in range(1, 5) if count % d == 0)
    kernel = lambda *refs: correlate_kernel(blocks, groups, *refs)
    out_shape = (count, local_chans, 2, TB, TB)
    return pl.pallas_call(
        kernel,
        out_shape=jax.ShapeDtypeStruct(out_shape, jnp.float32),
        in_specs=[
            pl.BlockSpec(memory_space=pltpu.SMEM),
            pl.BlockSpec(memory_space=pltpu.VMEM),
            pl.BlockSpec(memory_space=pltpu.VMEM),
        ],
        out_specs=pl.BlockSpec(memory_space=pl.ANY),
        scratch_shapes=[pltpu.VMEM(out_shape, jnp.float32), pltpu.SemaphoreType.DMA((groups,))],
        compiler_params=pltpu.CompilerParams(vmem_limit_bytes=48 * 1024 * 1024),
        cost_estimate=pl.CostEstimate(
            flops=2 * count * local_chans * 2 * TB * TB * depth,
            transcendentals=0,
            bytes_accessed=count * local_chans * 2 * TB * TB * 4 + lhs.size * 2 + spectra.size * 2,
        ),
    )(tile_ids, lhs, spectra)


def on_device(voltages, tile_map):
    local_inputs = voltages.shape[0]
    time_steps = voltages.shape[1]
    freq_devices = lax.axis_size("freq")
    time_devices = lax.axis_size("tm")
    channels = CH_DEV * freq_devices
    first_channel = NCHAN // 2 - channels // 2
    proto = prototype_rows()
    first, turn = phase_tables(first_channel, channels)
    if time_devices == 1:
        spectra = tap_products(voltages, proto, first, turn, channels, True)
    else:
        products = tap_products(voltages, proto, first, turn, channels, False)
        products = products.reshape(local_inputs, time_steps, TAPS, 2 * channels)
        tail = products[:, time_steps - (TAPS - 1) :]
        previous = passed_along(tail, "tm", 1)
        total = None
        for tap in range(TAPS):
            lead = TAPS - 1 - tap
            shifted = jnp.concatenate(
                [previous[:, tap:, tap], products[:, : time_steps - lead, tap]], axis=1
            )
            total = shifted if total is None else total + shifted
        spectra = total.reshape(local_inputs * time_steps, 2, channels).transpose(2, 1, 0)
        spectra = spectra.astype(jnp.bfloat16)
    spectra = spectra.reshape(freq_devices, CH_DEV, 2, local_inputs * time_steps)
    turned = lax.all_to_all(spectra, "freq", split_axis=0, concat_axis=0, tiled=True)
    slot_count = tile_map.shape[0] // time_devices
    inverse_count = 1.0 / (time_steps * time_devices)
    tile_ids = lax.dynamic_slice_in_dim(tile_map, lax.axis_index("tm") * slot_count, slot_count)
    arranged = arrange_rows(lax.all_gather(turned[None], "tm", axis=0, tiled=True), time_steps)
    arranged = arranged.reshape(arranged.shape[0], -1, arranged.shape[3])
    return tile_products(arranged, tile_ids, inverse_count)


def solution(mesh):
    in_specs = (P("freq", "tm", None, None), P())
    out_specs = P("tm", "freq", None, None, None)
    return jax.shard_map(
        on_device, mesh=mesh, in_specs=in_specs, out_specs=out_specs, check_vma=False
    )
```

```python
import math

import jax
import jax.numpy as jnp
from jax import lax
from jax.experimental import pallas as pl
from jax.experimental.pallas import tpu as pltpu
from jax.sharding import PartitionSpec as P

NCHAN = 4096
TAPS = 4
TB = 128
CH_DEV = 2
C_BLOCK = 2048
LANES = 128


def passed_along(value, axis, steps):
    count = lax.axis_size(axis)
    leading, last = (max(0, -steps), min(count, count - steps))
    return lax.ppermute(value, axis, [(source, source + steps) for source in range(leading, last)])


def channelize_kernel(
    channels,
    first_channel,
    fold_shift,
    x_hbm,
    out_ref,
    buf,
    sems,
    acc_ref,
    proto_ref,
    first_ref,
    turn_ref,
    *scratch,
):
    step = pl.program_id(0)
    count = pl.num_programs(0)
    cb = buf.shape[-1]

    def fetch(block, slot):
        for part in range(2):
            pltpu.make_async_copy(
                x_hbm.at[:, :, part, pl.ds(block * cb, cb)], buf.at[slot, part], sems.at[slot, part]
            ).start()

    @pl.when(step == 0)
    def _():
        fetch(0, 0)
        sample = (
            lax.broadcasted_iota(jnp.int32, proto_ref.shape, 0) * NCHAN
            + lax.broadcasted_iota(jnp.int32, proto_ref.shape, 1)
        ).astype(jnp.float32)
        position = (sample + 0.5) / NCHAN - TAPS / 2.0
        hann_taper = 0.5 - 0.5 * jnp.cos((sample + 0.5) * (2.0 * math.pi / (TAPS * NCHAN)))
        pi_x = math.pi * position
        proto_ref[...] = jnp.sin(pi_x) / pi_x * hann_taper / (128.0 * math.sqrt(NCHAN))
        angle = 2.0 * math.pi / NCHAN
        row = lax.broadcasted_iota(jnp.int32, (channels, LANES), 0) + first_channel
        lane = lax.broadcasted_iota(jnp.int32, (channels, LANES), 1)
        start = jnp.bitwise_and(lane * row, NCHAN - 1).astype(jnp.float32) * angle
        first_ref[:channels] = jnp.cos(start)
        first_ref[channels:] = jnp.sin(start)
        chunks = turn_ref.shape[0]
        chunk = lax.broadcasted_iota(jnp.int32, (chunks, channels), 0) * LANES
        col = lax.broadcasted_iota(jnp.int32, (chunks, channels), 1) + first_channel
        shift = jnp.bitwise_and(chunk * col, NCHAN - 1).astype(jnp.float32) * angle
        turn_ref[:, :channels] = jnp.cos(shift)
        turn_ref[:, channels:] = jnp.sin(shift)

    @pl.when(step + 1 < count)
    def _():
        fetch(step + 1, (step + 1) % 2)

    slot = step % 2
    for part in range(2):
        pltpu.make_async_copy(
            x_hbm.at[:, :, part, pl.ds(0, cb)], buf.at[slot, part], sems.at[slot, part]
        ).wait()
    per_block = cb // LANES
    turn = turn_ref[pl.ds(pl.multiple_of(step * per_block, per_block), per_block), :].T
    cos_0, sin_0 = first_ref[:channels], first_ref[channels:]
    cos_parts, sin_parts = [], []
    for chunk in range(cb // LANES):
        cos_t = jnp.broadcast_to(turn[:channels, chunk : chunk + 1], cos_0.shape)
        sin_t = jnp.broadcast_to(turn[channels:, chunk : chunk + 1], cos_0.shape)
        cos_parts.append(cos_0 * cos_t - sin_0 * sin_t)
        sin_parts.append(sin_0 * cos_t + cos_0 * sin_t)
    cosine = jnp.concatenate(cos_parts, axis=1)
    sine = jnp.concatenate(sin_parts, axis=1)
    upper = jnp.concatenate([cosine, -sine], axis=0)
    lower = jnp.concatenate([sine, cosine], axis=0)
    weights = proto_ref[:, pl.ds(pl.multiple_of(step * cb, cb), cb)]
    re_tables = []
    im_tables = []
    for tap in range(TAPS):
        w = weights[tap : tap + 1, :]
        re_tables.append((w * upper).astype(jnp.bfloat16))
        im_tables.append((w * lower).astype(jnp.bfloat16))
    re_table = jnp.concatenate(re_tables, axis=0)
    im_table = jnp.concatenate(im_tables, axis=0)
    rows = buf.shape[2] * buf.shape[3]
    x_re = buf[slot, 0].reshape(rows, cb).astype(jnp.bfloat16)
    x_im = buf[slot, 1].reshape(rows, cb).astype(jnp.bfloat16)
    dims = (((1,), (1,)), ((), ()))
    part = lax.dot_general(x_re, re_table, dims, preferred_element_type=jnp.float32) + lax.dot_general(
        x_im, im_table, dims, preferred_element_type=jnp.float32
    )

    @pl.when(step == 0)
    def _():
        acc_ref[...] = part

    @pl.when(jnp.logical_and(step > 0, step < count - 1))
    def _():
        acc_ref[...] += part

    @pl.when(step == count - 1)
    def _():
        products = acc_ref[...] + part
        if not fold_shift:
            out_ref[...] = products
            return
        time_steps = buf.shape[3]
        width = 2 * channels
        block = lax.broadcasted_iota(jnp.int32, (rows, width), 0) % time_steps
        total = None
        for tap in range(TAPS):
            term = products[:, tap * width : (tap + 1) * width]
            lead = TAPS - 1 - tap
            if lead:
                term = jnp.where(block >= lead, pltpu.roll(term, lead, 0), 0.0)
            total = term if total is None else total + term
        (staged,) = scratch
        lanes = staged.shape[-1]
        for half in range(2):
            rows_q = pl.ds(half, channels, stride=2)
            flipped = total[:, half * channels : (half + 1) * channels].T
            for chunk in range(staged.shape[0]):
                staged[chunk, rows_q, :] = flipped[:, chunk * lanes : (chunk + 1) * lanes]
        for chunk in range(staged.shape[0]):
            out_ref[:, chunk * lanes : (chunk + 1) * lanes] = staged[chunk].astype(out_ref.dtype)


def tap_products(voltages, first_channel, channels, fold_shift):
    local_inputs, time_steps = voltages.shape[0], voltages.shape[1]
    rows = local_inputs * time_steps
    width = TAPS * 2 * channels
    blocks = NCHAN // C_BLOCK
    kernel = lambda *refs: channelize_kernel(channels, first_channel, fold_shift, *refs)
    if fold_shift:
        out_shape = jax.ShapeDtypeStruct((2 * channels, rows), jnp.bfloat16)
    else:
        out_shape = jax.ShapeDtypeStruct((rows, width), jnp.float32)
    return pl.pallas_call(
        kernel,
        out_shape=out_shape,
        grid=(blocks,),
        in_specs=[pl.BlockSpec(memory_space=pl.ANY)],
        out_specs=pl.BlockSpec(out_shape.shape, lambda j: (0, 0)),
        scratch_shapes=[
            pltpu.VMEM((2, 2, local_inputs, time_steps, C_BLOCK), jnp.int32),
            pltpu.SemaphoreType.DMA((2, 2)),
            pltpu.VMEM((rows, width), jnp.float32),
            pltpu.VMEM((TAPS, NCHAN), jnp.float32),
            pltpu.VMEM((2 * channels, LANES), jnp.float32),
            pltpu.VMEM((NCHAN // LANES, 2 * channels), jnp.float32),
        ]
        + ([pltpu.VMEM((rows // 128, 2 * channels, 128), jnp.float32)] if fold_shift else []),
        compiler_params=pltpu.CompilerParams(
            dimension_semantics=("arbitrary",), vmem_limit_bytes=48 * 1024 * 1024
        ),
        cost_estimate=pl.CostEstimate(
            flops=2 * rows * 2 * NCHAN * width,
            transcendentals=0,
            bytes_accessed=voltages.size * 4 + rows * width * 4,
        ),
    )(voltages)


def tile_coords(tile_id, blocks):
    step_row = jnp.arange(1, blocks, dtype=jnp.int32)
    triangle = step_row * (step_row + 1) // 2
    row_block = jnp.sum((tile_id[..., None] >= triangle).astype(jnp.int32), axis=-1)
    col_block = tile_id - row_block * (row_block + 1) // 2
    return (row_block, col_block)


def arrange_rows(gathered, time_steps):
    piece_count = gathered.shape[0]
    freq_count = gathered.shape[1]
    local_chans = gathered.shape[2]
    inner_width = gathered.shape[4] // time_steps
    unfolded = gathered.reshape(piece_count, freq_count, local_chans, 2, inner_width, time_steps)
    unfolded = unfolded.transpose(2, 3, 0, 5, 1, 4)
    return unfolded.reshape(local_chans, 2, piece_count * time_steps, freq_count * inner_width)


def correlate_kernel(blocks, groups, ids_ref, lhs_ref, rhs_ref, out_hbm, staged, sems):
    count = staged.shape[0]
    per_group = count // groups

    def copy(group):
        part = pl.ds(group * per_group, per_group)
        return pltpu.make_async_copy(staged.at[part], out_hbm.at[part], sems.at[group])

    for group in range(groups):
        for slot in range(group * per_group, (group + 1) * per_group):
            tile_id = ids_ref[slot]
            row_block = jnp.int32(0)
            for r in range(1, blocks):
                row_block = row_block + (tile_id >= r * (r + 1) // 2).astype(jnp.int32)
            col_block = tile_id - row_block * (row_block + 1) // 2
            rows = pl.ds(pl.multiple_of(row_block * TB, TB), TB)
            cols = pl.ds(pl.multiple_of(col_block * TB, TB), TB)
            for chan in range(lhs_ref.shape[0]):
                right = rhs_ref[chan, :, cols]
                for part in range(2):
                    left = lhs_ref[chan, part, rows, :]
                    staged[slot, chan, part] = jnp.dot(left, right, preferred_element_type=jnp.float32)
        copy(group).start()
    for group in range(groups):
        copy(group).wait()


def tile_products(spectra, tile_ids, scale):
    local_chans, depth, paths = spectra.shape
    blocks = paths // TB
    half = depth // 2
    turned_rows = spectra.transpose(0, 2, 1)
    rotated = jnp.concatenate([turned_rows[:, :, half:], -turned_rows[:, :, :half]], axis=2)
    lhs = (jnp.stack([turned_rows, rotated], axis=1) * scale).astype(spectra.dtype)
    count = tile_ids.shape[0]
    groups = max(d for d in range(1, 5) if count % d == 0)
    kernel = lambda *refs: correlate_kernel(blocks, groups, *refs)
    out_shape = (count, local_chans, 2, TB, TB)
    return pl.pallas_call(
        kernel,
        out_shape=jax.ShapeDtypeStruct(out_shape, jnp.float32),
        in_specs=[
            pl.BlockSpec(memory_space=pltpu.SMEM),
            pl.BlockSpec(memory_space=pltpu.VMEM),
            pl.BlockSpec(memory_space=pltpu.VMEM),
        ],
        out_specs=pl.BlockSpec(memory_space=pl.ANY),
        scratch_shapes=[pltpu.VMEM(out_shape, jnp.float32), pltpu.SemaphoreType.DMA((groups,))],
        compiler_params=pltpu.CompilerParams(vmem_limit_bytes=48 * 1024 * 1024),
        cost_estimate=pl.CostEstimate(
            flops=2 * count * local_chans * 2 * TB * TB * depth,
            transcendentals=0,
            bytes_accessed=count * local_chans * 2 * TB * TB * 4 + lhs.size * 2 + spectra.size * 2,
        ),
    )(tile_ids, lhs, spectra)


def on_device(voltages, tile_map):
    local_inputs = voltages.shape[0]
    time_steps = voltages.shape[1]
    freq_devices = lax.axis_size("freq")
    time_devices = lax.axis_size("tm")
    channels = CH_DEV * freq_devices
    first_channel = NCHAN // 2 - channels // 2
    if time_devices == 1:
        spectra = tap_products(voltages, first_channel, channels, True)
    else:
        products = tap_products(voltages, first_channel, channels, False)
        products = products.reshape(local_inputs, time_steps, TAPS, 2 * channels)
        tail = products[:, time_steps - (TAPS - 1) :]
        previous = passed_along(tail, "tm", 1)
        total = None
        for tap in range(TAPS):
            lead = TAPS - 1 - tap
            shifted = jnp.concatenate(
                [previous[:, tap:, tap], products[:, : time_steps - lead, tap]], axis=1
            )
            total = shifted if total is None else total + shifted
        spectra = total.reshape(local_inputs * time_steps, 2, channels).transpose(2, 1, 0)
        spectra = spectra.astype(jnp.bfloat16)
    spectra = spectra.reshape(freq_devices, CH_DEV, 2, local_inputs * time_steps)
    turned = lax.all_to_all(spectra, "freq", split_axis=0, concat_axis=0, tiled=True)
    slot_count = tile_map.shape[0] // time_devices
    inverse_count = 1.0 / (time_steps * time_devices)
    tile_ids = lax.dynamic_slice_in_dim(tile_map, lax.axis_index("tm") * slot_count, slot_count)
    arranged = arrange_rows(lax.all_gather(turned[None], "tm", axis=0, tiled=True), time_steps)
    arranged = arranged.reshape(arranged.shape[0], -1, arranged.shape[3])
    return tile_products(arranged, tile_ids, inverse_count)


def solution(mesh):
    in_specs = (P("freq", "tm", None, None), P())
    out_specs = P("tm", "freq", None, None, None)
    return jax.shard_map(
        on_device, mesh=mesh, in_specs=in_specs, out_specs=out_specs, check_vma=False
    )
```
